1024 devices in a mesh: dp: 8 (over x), seq: 8 (over z), enc: 16 (over y, core).
Axes of the slice: x: 8, y: 8, z: 8, core: 2. Of those that a mesh axis runs over, the one named last changes fastest.
Arguments:
- queries: bfloat16 [128, 1024, 2048], P(('dp', 'enc'), 'seq'), may hold values from -12 to 12
- cotangent: bfloat16 [128, 1024, 2048], P(('dp', 'enc'), 'seq'), may hold values from -12 to 12
- key_pool: bfloat16 [8, 8, 8, 128, 2048], P('dp', 'seq', None, None, 'enc'), may hold values from -12 to 12
- value_pool: bfloat16 [8, 8, 8, 128, 2048], P('dp', 'seq', None, None, 'enc'), may hold values from -6 to 6
- counts: int32 [128, 16], P('dp', 'seq'), may hold values from 0 to 4
- neighbour_ids: int32 [128, 16, 4], P('dp', 'seq'), may hold values from 0 to 7, all different within a row
- rel_bias: float32 [16, 191], P('enc'), may hold values from -3 to 3
Outputs:
- context: bfloat16 [128, 1024, 2048], P(('dp', 'enc'), 'seq')
- query_grad: bfloat16 [128, 1024, 2048], P(('dp', 'enc'), 'seq')
- key_grad: bfloat16 [8, 8, 8, 128, 2048], P('dp', 'seq', None, None, 'enc')
- value_grad: bfloat16 [8, 8, 8, 128, 2048], P('dp', 'seq', None, None, 'enc')
- bias_grad: float32 [16, 191], P('enc')
The draws below stay inside these ranges and needn't reach their ends.
Inputs may be any that keep to these rules, and one draw needn't show every extreme that they name: Only the first counts[c] ids of a block are used. `neighbour_ids`: the 4 ids of one block are distinct.
All inputs are finite; a program needn't handle non-finite values.
Results may differ from the reference program's by a relative error of at most 0.0085.
Values may be sent and summed in bfloat16 or wider, within the bound.
No kernel may reach another device: no remote copies, remote signals or barrier semaphores. Data moves between devices by JAX's collectives and lax.ppermute only.
A program may use at most 64 MiB of HBM per device.

```python
import math
import jax
import jax.numpy as jnp
from jax import lax

HEAD_DIM = 128
BLOCK_LEN = 64
PASSAGE = 128
NEIGHBOURS = 4
TOK_DEV = 128
POOL = 8
HEADS = 16
SEQS = 128
LENGTH = 1024
BLOCKS_SEQ = 16
REL = 191
DATA_GROUPS = 8
SPANS = 8
N_DP = 8
N_SEQ = 8
N_ENC = 16


def draw_queries(key, part):
    base = jax.random.truncated_normal(jax.random.fold_in(key, 1), -6.0, 6.0, (SEQS, LENGTH, HEADS, HEAD_DIM), jnp.float32)
    return base.reshape(SEQS, LENGTH, HEADS * HEAD_DIM).astype(jnp.bfloat16)


def draw_key_pool(key, part):
    base = jax.random.truncated_normal(jax.random.fold_in(key, 2), -6.0, 6.0, (DATA_GROUPS, SPANS, POOL, PASSAGE, HEADS, HEAD_DIM), jnp.float32)
    return base.reshape(DATA_GROUPS, SPANS, POOL, PASSAGE, HEADS * HEAD_DIM).astype(jnp.bfloat16)


def set_ends(values, stream_key, least, high):
    dims = values.shape
    index_at = [jax.random.randint(jax.random.fold_in(stream_key, axis), (), 0, dims[axis]) for axis in range(len(dims))]
    values = values.at[tuple(index_at)].set(least)
    longest = dims.index(max(dims))
    index_at[longest] = (index_at[longest] + 1) % dims[longest]
    return values.at[tuple(index_at)].set(high)


def block_levels(own_key, extent, split, low, top_value):
    level, own = 1.0, jax.random.fold_in(own_key, 6)
    for axis_at, blocks in split:
        steps = jnp.exp(jax.random.uniform(jax.random.fold_in(own, axis_at), (blocks,), jnp.float32, low / len(split), top_value / len(split)))
        level = level * jnp.repeat(steps, extent[axis_at] // blocks).reshape([-1 if axis == axis_at else 1 for axis in range(len(extent))])
    return level


def picks_of(rng, rows, amount, top, lift):
    sequence = jax.random.permutation(jax.random.fold_in(rng, 1), amount)
    favour = sequence
    for power in range(3):
        favour = favour * favour // amount
    favour = favour * lift // amount
    tickets = jax.random.randint(jax.random.fold_in(rng, 2), (rows, amount), 0, 4096) + favour
    holders = jax.random.permutation(jax.random.fold_in(rng, 3), rows)[jnp.arange(amount) % rows]
    tickets = jnp.where(jnp.arange(rows)[:, None] == holders[None, :], 1 << 14, tickets)
    priority = tickets * amount + jnp.arange(amount)
    return lax.top_k(priority.astype(jnp.int32), top)[1].astype(jnp.int32)


def noise(own_key, dims, scale, limit, cuts=(), kind=jnp.bfloat16):
    result = jax.random.normal(own_key, dims, jnp.float32) * scale
    if len(cuts) > 0:
        result = block_levels(own_key, dims, cuts, -0.22, 0.18) * result
    return jnp.clip(result, min=-limit, max=limit).astype(kind)


def setup_inputs(seed: int = 0) -> dict:
    streams_of = jax.random.split(jax.random.key(seed), 8)
    queries = draw_queries(jax.random.fold_in(streams_of[7], 71), 0)
    cotangent = noise(streams_of[1], (SEQS, LENGTH, HEADS * HEAD_DIM), 2.0, 12.0, ((0, 128), (1, 8)))
    key_pool = draw_key_pool(jax.random.fold_in(streams_of[7], 71), 0)
    value_pool = noise(streams_of[3], (DATA_GROUPS, SPANS, POOL, PASSAGE, HEADS * HEAD_DIM), 1.0, 6.0, ((0, 8), (1, 8), (4, 16)))
    counts = set_ends(jax.random.randint(streams_of[4], (SEQS, BLOCKS_SEQ), 0, NEIGHBOURS + 1), jax.random.fold_in(streams_of[4], 1), 0, NEIGHBOURS).astype(jnp.int32)
    neighbour_ids = picks_of(streams_of[5], SEQS * BLOCKS_SEQ, POOL, NEIGHBOURS, 0).reshape((SEQS, BLOCKS_SEQ, NEIGHBOURS))
    rel_bias = noise(streams_of[6], (HEADS, REL), 0.5, 3.0, ((0, 16),), jnp.float32)
    return dict(queries=queries, cotangent=cotangent, key_pool=key_pool, value_pool=value_pool, counts=counts, neighbour_ids=neighbour_ids, rel_bias=rel_bias)


NEG_FILL = -1e+30

def one_item(pieces):
    query_rows, grad_rows, pool_keys, pool_values, block_counts, block_ids, bias_line = pieces
    score_scale = 1.0 / math.sqrt(HEAD_DIM)
    offsets = (jnp.arange(PASSAGE)[None, :] - jnp.arange(BLOCK_LEN)[:, None] + BLOCK_LEN - 1).astype(jnp.int32)
    row_bias = bias_line[offsets]
    keys_sel = pool_keys[block_ids].astype(jnp.float32)
    values_sel = pool_values[block_ids].astype(jnp.float32)
    query_f = query_rows.astype(jnp.float32)
    grad_f = grad_rows.astype(jnp.float32)
    scores = jnp.einsum('cqd,cjtd->cqjt', query_f, keys_sel) * score_scale + row_bias[None, :, None, :]
    usable = (jnp.arange(NEIGHBOURS)[None, :] < block_counts[:, None])[:, None, :, None]
    row_top = lax.optimization_barrier(jnp.max(jnp.where(usable, scores, NEG_FILL), axis=(2, 3), keepdims=True))
    raised = jnp.where(usable, jnp.exp(scores - row_top), 0.0)
    no_keys = (block_counts == 0).astype(jnp.float32)[:, None, None, None]
    weights = raised / (lax.optimization_barrier(jnp.sum(raised, axis=(2, 3), keepdims=True)) + no_keys)
    weights_low = lax.optimization_barrier(weights.astype(jnp.bfloat16)).astype(jnp.float32)
    context = jnp.einsum('cqjt,cjtd->cqd', weights_low, values_sel).astype(jnp.bfloat16)
    grad_weights = jnp.einsum('cqd,cjtd->cqjt', grad_f, values_sel)
    row_delta = lax.optimization_barrier(jnp.sum(weights * grad_weights, axis=(2, 3), keepdims=True))
    grad_scores = weights * (grad_weights - row_delta)
    scores_low = lax.optimization_barrier(grad_scores.astype(jnp.bfloat16)).astype(jnp.float32)
    query_grad = (score_scale * jnp.einsum('cqjt,cjtd->cqd', scores_low, keys_sel)).astype(jnp.bfloat16)
    selector = (block_ids[:, :, None] == jnp.arange(POOL).astype(jnp.int32)[None, None, :]).astype(jnp.float32)
    key_slots = jnp.einsum('cqjt,cqd->cjtd', scores_low, query_f)
    key_grad = (score_scale * jnp.einsum('cjn,cjtd->ntd', selector, key_slots, precision=lax.Precision.HIGHEST)).astype(jnp.bfloat16)
    value_slots = jnp.einsum('cqjt,cqd->cjtd', weights_low, grad_f)
    value_grad = jnp.einsum('cjn,cjtd->ntd', selector, value_slots, precision=lax.Precision.HIGHEST).astype(jnp.bfloat16)
    bias_part = jax.ops.segment_sum(lax.optimization_barrier(jnp.sum(grad_scores, axis=(0, 2))).reshape(-1), offsets.reshape(-1), num_segments=REL)
    return (context, query_grad, key_grad, value_grad, bias_part)

def reference(queries, cotangent, key_pool, value_pool, counts, neighbour_ids, rel_bias):
    blocks_dev = TOK_DEV // BLOCK_LEN
    group_blocks = N_ENC * blocks_dev
    groups = N_DP * N_SEQ

    def token_heads(source):
        shaped = source.reshape(N_DP, N_ENC, N_SEQ, blocks_dev, BLOCK_LEN, HEADS, HEAD_DIM)
        return shaped.transpose(0, 2, 5, 1, 3, 4, 6).reshape(groups * HEADS, group_blocks, BLOCK_LEN, HEAD_DIM)

    def pool_heads(source):
        shaped = source.reshape(N_DP, N_SEQ, POOL, PASSAGE, HEADS, HEAD_DIM)
        return shaped.transpose(0, 1, 4, 2, 3, 5).reshape(groups * HEADS, POOL, PASSAGE, HEAD_DIM)
    count_rows = counts.reshape(N_DP, N_ENC, N_SEQ, blocks_dev).transpose(0, 2, 1, 3).reshape(groups, group_blocks)
    count_rows = jnp.repeat(count_rows, HEADS, axis=0)
    id_rows = neighbour_ids.reshape(N_DP, N_ENC, N_SEQ, blocks_dev, NEIGHBOURS).transpose(0, 2, 1, 3, 4)
    id_rows = jnp.repeat(id_rows.reshape(groups, group_blocks, NEIGHBOURS), HEADS, axis=0)
    bias_rows = jnp.tile(rel_bias, (groups, 1))
    results = lax.map(one_item, (token_heads(queries), token_heads(cotangent), pool_heads(key_pool), pool_heads(value_pool), count_rows, id_rows, bias_rows))

    def back_tokens(source):
        shaped = source.reshape(N_DP, N_SEQ, HEADS, N_ENC, blocks_dev, BLOCK_LEN, HEAD_DIM)
        return shaped.transpose(0, 3, 1, 4, 5, 2, 6).reshape(SEQS, LENGTH, HEADS * HEAD_DIM)

    def back_pool(source):
        shaped = source.reshape(N_DP, N_SEQ, HEADS, POOL, PASSAGE, HEAD_DIM)
        return shaped.transpose(0, 1, 3, 4, 2, 5).reshape(N_DP, N_SEQ, POOL, PASSAGE, HEADS * HEAD_DIM)
    bias_grad = results[4].reshape(groups, HEADS, REL).sum(axis=0)
    return (back_tokens(results[0]), back_tokens(results[1]), back_pool(results[2]), back_pool(results[3]), bias_grad)
```

```python
import math

import jax
import jax.numpy as jnp
from jax import lax
from jax.sharding import PartitionSpec as P

HEAD_DIM = 128
BLOCK_LEN = 64
PASSAGE = 128


NEG_FILL = -1e30


def bias_rows(bias_table):
    heads_here, table_width = bias_table.shape
    padded = jnp.pad(bias_table, ((0, 0), (0, 1)))
    tiled_rows = jnp.broadcast_to(padded[:, None, :], (heads_here, BLOCK_LEN, table_width + 1))
    tiled_rows = tiled_rows.reshape(heads_here, BLOCK_LEN * (table_width + 1))[
        :, : BLOCK_LEN * table_width
    ]
    tiled_rows = tiled_rows.reshape(heads_here, BLOCK_LEN, table_width)
    return tiled_rows[:, :, BLOCK_LEN - 1 : BLOCK_LEN - 1 + PASSAGE]


def fold_bias(totals, table_width):
    heads_here = totals.shape[0]
    padded = jnp.pad(totals, ((0, 0), (0, 0), (BLOCK_LEN - 1, 0)))
    flat_rows = padded.reshape(heads_here, BLOCK_LEN * table_width)
    flat_rows = jnp.pad(flat_rows, ((0, 0), (0, BLOCK_LEN)))
    return flat_rows.reshape(heads_here, BLOCK_LEN, table_width + 1).sum(axis=1)[:, :table_width]


def attend_all(query_heads, grad_heads, id_table, count_table, pool_keys, pool_values, row_bias):
    score_scale = 1.0 / math.sqrt(HEAD_DIM)
    pool_size = pool_keys.shape[0]
    width = pool_size * PASSAGE
    keys_flat = pool_keys.reshape(width, HEAD_DIM)
    values_flat = pool_values.reshape(width, HEAD_DIM)
    slot_index = jnp.arange(id_table.shape[1])
    picked = (slot_index[None, :] < count_table[:, None])[:, :, None] & (
        id_table[:, :, None] == jnp.arange(pool_size)[None, None, :]
    )
    usable = jnp.repeat(jnp.any(picked, axis=1), PASSAGE, axis=1)[:, None, :]
    bias_wide = jnp.tile(row_bias[0], (1, pool_size))[None]
    scores = (
        jnp.einsum("cqd,kd->cqk", query_heads, keys_flat, preferred_element_type=jnp.float32)
        * score_scale
    )
    scores = scores + bias_wide
    row_top = jnp.max(jnp.where(usable, scores, NEG_FILL), axis=2, keepdims=True)
    raised = jnp.where(usable, jnp.exp(scores - row_top), 0.0)
    no_keys = (count_table == 0).astype(jnp.float32)[:, None, None]
    weights = raised / (jnp.sum(raised, axis=2, keepdims=True) + no_keys)
    weights_low = weights.astype(jnp.bfloat16)
    context = jnp.einsum(
        "cqk,kd->cqd", weights_low, values_flat, preferred_element_type=jnp.float32
    ).astype(jnp.bfloat16)
    grad_weights = jnp.einsum(
        "cqd,kd->cqk", grad_heads, values_flat, preferred_element_type=jnp.float32
    )
    row_delta = jnp.sum(weights * grad_weights, axis=2, keepdims=True)
    grad_scores = weights * (grad_weights - row_delta)
    scores_low = grad_scores.astype(jnp.bfloat16)
    query_grad = (
        score_scale
        * jnp.einsum("cqk,kd->cqd", scores_low, keys_flat, preferred_element_type=jnp.float32)
    ).astype(jnp.bfloat16)
    key_grad = score_scale * jnp.einsum(
        "cqk,cqd->kd", scores_low, query_heads, preferred_element_type=jnp.float32
    )
    value_grad = jnp.einsum(
        "cqk,cqd->kd", weights_low, grad_heads, preferred_element_type=jnp.float32
    )
    bias_total = jnp.sum(grad_scores, axis=0).reshape(BLOCK_LEN, pool_size, PASSAGE).sum(axis=1)
    return (context, query_grad, key_grad, value_grad, bias_total[None])


def reduce_groups(part):
    return lax.psum(lax.psum(part, "dp"), "seq")


def local(queries, cotangent, key_pool, value_pool, counts, neighbour_ids, rel_bias):
    token_rows = queries.shape[1]
    full_width = queries.shape[2]
    blocks_here = token_rows // BLOCK_LEN
    head_width = key_pool.shape[-1]
    heads_here = head_width // HEAD_DIM
    pool_size = key_pool.shape[2]
    pool_keys = key_pool.reshape(pool_size, PASSAGE, head_width)
    pool_values = value_pool.reshape(pool_size, PASSAGE, head_width)
    id_table = neighbour_ids.reshape(-1, neighbour_ids.shape[-1])
    count_table = counts.reshape(-1)
    row_bias = bias_rows(rel_bias)
    both_rows = jnp.stack(
        [
            queries.reshape(blocks_here, BLOCK_LEN, full_width),
            cotangent.reshape(blocks_here, BLOCK_LEN, full_width),
        ]
    )
    both_heads = lax.all_to_all(both_rows, "enc", split_axis=3, concat_axis=1, tiled=True)
    context_heads, query_part, key_total, value_total, bias_total = attend_all(
        both_heads[0], both_heads[1], id_table, count_table, pool_keys, pool_values, row_bias
    )
    both_back = lax.all_to_all(
        jnp.stack([context_heads, query_part]), "enc", split_axis=1, concat_axis=3, tiled=True
    )
    bias_grad = reduce_groups(fold_bias(bias_total, rel_bias.shape[1]))
    return (
        both_back[0].reshape(queries.shape),
        both_back[1].reshape(queries.shape),
        key_total.astype(jnp.bfloat16).reshape(key_pool.shape),
        value_total.astype(jnp.bfloat16).reshape(value_pool.shape),
        bias_grad,
    )


def solution(mesh):
    in_specs = (
        P(("dp", "enc"), "seq", None),
        P(("dp", "enc"), "seq", None),
        P("dp", "seq", None, None, "enc"),
        P("dp", "seq", None, None, "enc"),
        P("dp", "seq"),
        P("dp", "seq", None),
        P("enc", None),
    )
    out_specs = (
        P(("dp", "enc"), "seq", None),
        P(("dp", "enc"), "seq", None),
        P("dp", "seq", None, None, "enc"),
        P("dp", "seq", None, None, "enc"),
        P("enc", None),
    )
    return jax.shard_map(local, mesh=mesh, in_specs=in_specs, out_specs=out_specs, check_vma=False)
```

```python
import math

import jax
import jax.numpy as jnp
from jax import lax
from jax.experimental import pallas as pl
from jax.experimental.pallas import tpu as pltpu
from jax.sharding import PartitionSpec as P

HEAD_DIM = 128
BLOCK_LEN = 64
PASSAGE = 128


NEG_FILL = -1e30


def bias_rows(bias_table):
    heads_here, table_width = bias_table.shape
    padded = jnp.pad(bias_table, ((0, 0), (0, 1)))
    tiled_rows = jnp.broadcast_to(padded[:, None, :], (heads_here, BLOCK_LEN, table_width + 1))
    tiled_rows = tiled_rows.reshape(heads_here, BLOCK_LEN * (table_width + 1))[
        :, : BLOCK_LEN * table_width
    ]
    tiled_rows = tiled_rows.reshape(heads_here, BLOCK_LEN, table_width)
    return tiled_rows[:, :, BLOCK_LEN - 1 : BLOCK_LEN - 1 + PASSAGE]


def fold_bias(totals, table_width):
    heads_here = totals.shape[0]
    padded = jnp.pad(totals, ((0, 0), (0, 0), (BLOCK_LEN - 1, 0)))
    flat_rows = padded.reshape(heads_here, BLOCK_LEN * table_width)
    flat_rows = jnp.pad(flat_rows, ((0, 0), (0, BLOCK_LEN)))
    return flat_rows.reshape(heads_here, BLOCK_LEN, table_width + 1).sum(axis=1)[:, :table_width]


def attend_kernel(qd_ref, keys_ref, values_ref, bias_ref, mask_ref, out_ref, key_out, value_out,
                  bias_out, key_acc, value_acc, bias_acc):
    step = pl.program_id(0)
    score_scale = 1.0 / math.sqrt(HEAD_DIM)
    seqs_here, halves, rows_seq, _ = qd_ref.shape
    blocks_seq = rows_seq // BLOCK_LEN
    rows = seqs_here * rows_seq
    width = keys_ref.shape[0]
    tile4 = (seqs_here, blocks_seq, BLOCK_LEN, width)
    contract_last = (((1,), (1,)), ((), ()))
    contract_first = (((0,), (0,)), ((), ()))

    @pl.when(step == 0)
    def _():
        key_acc[...] = jnp.zeros_like(key_acc)
        value_acc[...] = jnp.zeros_like(value_acc)
        bias_acc[...] = jnp.zeros_like(bias_acc)

    query_rows = qd_ref[:, 0].reshape(rows, HEAD_DIM)
    grad_rows = qd_ref[:, 1].reshape(rows, HEAD_DIM)
    keys = keys_ref[...]
    values = values_ref[...]
    scores = lax.dot_general(query_rows, keys, contract_last, preferred_element_type=jnp.float32)
    scores = scores.reshape(tile4) * score_scale + bias_ref[...][None, None]
    usable = mask_ref[...][:, :, None, :] > 0.5
    row_top = jnp.max(jnp.where(usable, scores, NEG_FILL), axis=3, keepdims=True)
    raised = jnp.where(usable, jnp.exp(scores - row_top), 0.0)
    total = jnp.sum(raised, axis=3, keepdims=True)
    weights = raised / (total + jnp.where(total == 0.0, 1.0, 0.0))
    weights_low = weights.astype(jnp.bfloat16).reshape(rows, width)
    context = jnp.dot(weights_low, values, preferred_element_type=jnp.float32)
    grad_weights = lax.dot_general(grad_rows, values, contract_last, preferred_element_type=jnp.float32)
    grad_weights = grad_weights.reshape(tile4)
    row_delta = jnp.sum(weights * grad_weights, axis=3, keepdims=True)
    grad_scores = weights * (grad_weights - row_delta)
    scores_low = grad_scores.astype(jnp.bfloat16).reshape(rows, width)
    query_grad = score_scale * jnp.dot(scores_low, keys, preferred_element_type=jnp.float32)
    out_ref[:, 0] = context.astype(jnp.bfloat16).reshape(seqs_here, rows_seq, HEAD_DIM)
    out_ref[:, 1] = query_grad.astype(jnp.bfloat16).reshape(seqs_here, rows_seq, HEAD_DIM)
    key_acc[...] += lax.dot_general(scores_low, query_rows, contract_first, preferred_element_type=jnp.float32)
    value_acc[...] += lax.dot_general(weights_low, grad_rows, contract_first, preferred_element_type=jnp.float32)
    bias_acc[...] += jnp.sum(grad_scores, axis=(0, 1))

    @pl.when(step == pl.num_programs(0) - 1)
    def _():
        key_out[...] = (score_scale * key_acc[...]).astype(key_out.dtype)
        value_out[...] = value_acc[...].astype(value_out.dtype)
        folded = bias_acc[:, 0:PASSAGE]
        for part in range(1, width // PASSAGE):
            folded = folded + bias_acc[:, part * PASSAGE:(part + 1) * PASSAGE]
        bias_out[...] = folded


def attend_all(both_heads, id_table, count_table, pool_keys, pool_values, row_bias):
    seq_total, halves, rows_seq, _ = both_heads.shape
    pool_size = pool_keys.shape[0]
    width = pool_size * PASSAGE
    blocks_seq = rows_seq // BLOCK_LEN
    keys_flat = pool_keys.reshape(width, HEAD_DIM)
    values_flat = pool_values.reshape(width, HEAD_DIM)
    slot_index = jnp.arange(id_table.shape[1])
    picked = (slot_index[None, :] < count_table[:, None])[:, :, None] & (
        id_table[:, :, None] == jnp.arange(pool_size)[None, None, :]
    )
    usable = jnp.repeat(jnp.any(picked, axis=1).astype(jnp.float32), PASSAGE, axis=1)
    usable = usable.reshape(seq_total, blocks_seq, width)
    bias_wide = jnp.tile(row_bias[0], (1, pool_size))
    seqs_step = 2
    grid = (seq_total // seqs_step,)
    return pl.pallas_call(
        attend_kernel,
        grid=grid,
        in_specs=[
            pl.BlockSpec((seqs_step, halves, rows_seq, HEAD_DIM), lambda i: (i, 0, 0, 0)),
            pl.BlockSpec((width, HEAD_DIM), lambda i: (0, 0)),
            pl.BlockSpec((width, HEAD_DIM), lambda i: (0, 0)),
            pl.BlockSpec((BLOCK_LEN, width), lambda i: (0, 0)),
            pl.BlockSpec((seqs_step, blocks_seq, width), lambda i: (i, 0, 0)),
        ],
        out_specs=[
            pl.BlockSpec((seqs_step, halves, rows_seq, HEAD_DIM), lambda i: (i, 0, 0, 0)),
            pl.BlockSpec((width, HEAD_DIM), lambda i: (0, 0)),
            pl.BlockSpec((width, HEAD_DIM), lambda i: (0, 0)),
            pl.BlockSpec((BLOCK_LEN, PASSAGE), lambda i: (0, 0)),
        ],
        out_shape=[
            jax.ShapeDtypeStruct(both_heads.shape, jnp.bfloat16),
            jax.ShapeDtypeStruct((width, HEAD_DIM), jnp.bfloat16),
            jax.ShapeDtypeStruct((width, HEAD_DIM), jnp.bfloat16),
            jax.ShapeDtypeStruct((BLOCK_LEN, PASSAGE), jnp.float32),
        ],
        scratch_shapes=[
            pltpu.VMEM((width, HEAD_DIM), jnp.float32),
            pltpu.VMEM((width, HEAD_DIM), jnp.float32),
            pltpu.VMEM((BLOCK_LEN, width), jnp.float32),
        ],
        compiler_params=pltpu.CompilerParams(dimension_semantics=("arbitrary",)),
    )(both_heads, keys_flat, values_flat, bias_wide, usable)


def reduce_groups(part):
    return lax.psum(lax.psum(part, "dp"), "seq")


def local(queries, cotangent, key_pool, value_pool, counts, neighbour_ids, rel_bias):
    token_rows = queries.shape[1]
    full_width = queries.shape[2]
    blocks_here = token_rows // BLOCK_LEN
    head_width = key_pool.shape[-1]
    heads_total = full_width // HEAD_DIM
    pool_size = key_pool.shape[2]
    pool_keys = key_pool.reshape(pool_size, PASSAGE, head_width)
    pool_values = value_pool.reshape(pool_size, PASSAGE, head_width)
    id_table = neighbour_ids.reshape(-1, neighbour_ids.shape[-1])
    count_table = counts.reshape(-1)
    row_bias = bias_rows(rel_bias)
    both_rows = jnp.stack(
        [
            queries.reshape(token_rows, heads_total, HEAD_DIM),
            cotangent.reshape(token_rows, heads_total, HEAD_DIM),
        ]
    ).transpose(2, 0, 1, 3)
    both_heads = lax.all_to_all(both_rows, "enc", split_axis=0, concat_axis=0, tiled=True)
    both_out, key_total, value_total, bias_total = attend_all(
        both_heads, id_table, count_table, pool_keys, pool_values, row_bias
    )
    both_back = lax.all_to_all(both_out, "enc", split_axis=0, concat_axis=0, tiled=True)
    both_back = both_back.transpose(1, 2, 0, 3).reshape((2,) + queries.shape)
    bias_grad = reduce_groups(fold_bias(bias_total[None], rel_bias.shape[1]))
    return (
        both_back[0],
        both_back[1],
        key_total.reshape(key_pool.shape),
        value_total.reshape(value_pool.shape),
        bias_grad,
    )


def solution(mesh):
    in_specs = (
        P(("dp", "enc"), "seq", None),
        P(("dp", "enc"), "seq", None),
        P("dp", "seq", None, None, "enc"),
        P("dp", "seq", None, None, "enc"),
        P("dp", "seq"),
        P("dp", "seq", None),
        P("enc", None),
    )
    out_specs = (
        P(("dp", "enc"), "seq", None),
        P(("dp", "enc"), "seq", None),
        P("dp", "seq", None, None, "enc"),
        P("dp", "seq", None, None, "enc"),
        P("enc", None),
    )
    return jax.shard_map(local, mesh=mesh, in_specs=in_specs, out_specs=out_specs, check_vma=False)
```

```python
import functools
import math

import jax
import jax.numpy as jnp
from jax import lax
from jax.experimental import pallas as pl
from jax.experimental.pallas import tpu as pltpu
from jax.sharding import PartitionSpec as P

HEAD_DIM = 128
BLOCK_LEN = 64
PASSAGE = 128


NEG_FILL = -1e30


def bias_rows(bias_table):
    heads_here, table_width = bias_table.shape
    padded = jnp.pad(bias_table, ((0, 0), (0, 1)))
    tiled_rows = jnp.broadcast_to(padded[:, None, :], (heads_here, BLOCK_LEN, table_width + 1))
    tiled_rows = tiled_rows.reshape(heads_here, BLOCK_LEN * (table_width + 1))[
        :, : BLOCK_LEN * table_width
    ]
    tiled_rows = tiled_rows.reshape(heads_here, BLOCK_LEN, table_width)
    return tiled_rows[:, :, BLOCK_LEN - 1 : BLOCK_LEN - 1 + PASSAGE]


def fold_bias(totals, table_width):
    heads_here = totals.shape[0]
    padded = jnp.pad(totals, ((0, 0), (0, 0), (BLOCK_LEN - 1, 0)))
    flat_rows = padded.reshape(heads_here, BLOCK_LEN * table_width)
    flat_rows = jnp.pad(flat_rows, ((0, 0), (0, BLOCK_LEN)))
    return flat_rows.reshape(heads_here, BLOCK_LEN, table_width + 1).sum(axis=1)[:, :table_width]


def attend_kernel(qd_ref, keys_ref, values_ref, bias_ref, mask_ref, out_ref, key_out, value_out,
                  bias_out, key_acc, value_acc, bias_acc):
    step = pl.program_id(0)
    score_scale = 1.0 / math.sqrt(HEAD_DIM)
    seqs_here, halves, rows_seq, _ = qd_ref.shape
    blocks_seq = rows_seq // BLOCK_LEN
    rows = seqs_here * rows_seq
    width = keys_ref.shape[0]
    tile4 = (seqs_here, blocks_seq, BLOCK_LEN, width)
    contract_last = (((1,), (1,)), ((), ()))
    contract_first = (((0,), (0,)), ((), ()))

    @pl.when(step == 0)
    def _():
        key_acc[...] = jnp.zeros_like(key_acc)
        value_acc[...] = jnp.zeros_like(value_acc)
        bias_acc[...] = jnp.zeros_like(bias_acc)

    query_rows = qd_ref[:, 0].reshape(rows, HEAD_DIM)
    grad_rows = qd_ref[:, 1].reshape(rows, HEAD_DIM)
    keys = keys_ref[...]
    values = values_ref[...]
    scores = lax.dot_general(query_rows, keys, contract_last, preferred_element_type=jnp.float32)
    scores = scores.reshape(tile4) * score_scale + bias_ref[...][None, None]
    usable = mask_ref[...][:, :, None, :] > 0.5
    row_top = jnp.max(jnp.where(usable, scores, NEG_FILL), axis=3, keepdims=True)
    raised = jnp.where(usable, jnp.exp(scores - row_top), 0.0)
    total = jnp.sum(raised, axis=3, keepdims=True)
    weights = raised / (total + jnp.where(total == 0.0, 1.0, 0.0))
    weights_low = weights.astype(jnp.bfloat16).reshape(rows, width)
    context = jnp.dot(weights_low, values, preferred_element_type=jnp.float32)
    grad_weights = lax.dot_general(grad_rows, values, contract_last, preferred_element_type=jnp.float32)
    grad_weights = grad_weights.reshape(tile4)
    row_delta = jnp.sum(weights * grad_weights, axis=3, keepdims=True)
    grad_scores = weights * (grad_weights - row_delta)
    scores_low = grad_scores.astype(jnp.bfloat16).reshape(rows, width)
    query_grad = score_scale * jnp.dot(scores_low, keys, preferred_element_type=jnp.float32)
    out_ref[:, 0] = context.astype(jnp.bfloat16).reshape(seqs_here, rows_seq, HEAD_DIM)
    out_ref[:, 1] = query_grad.astype(jnp.bfloat16).reshape(seqs_here, rows_seq, HEAD_DIM)
    key_acc[...] += lax.dot_general(scores_low, query_rows, contract_first, preferred_element_type=jnp.float32)
    value_acc[...] += lax.dot_general(weights_low, grad_rows, contract_first, preferred_element_type=jnp.float32)
    bias_acc[...] += jnp.sum(grad_scores, axis=(0, 1))

    @pl.when(step == pl.num_programs(0) - 1)
    def _():
        key_out[...] = (score_scale * key_acc[...]).astype(key_out.dtype)
        value_out[...] = value_acc[...].astype(value_out.dtype)
        folded = bias_acc[:, 0:PASSAGE]
        for part in range(1, width // PASSAGE):
            folded = folded + bias_acc[:, part * PASSAGE:(part + 1) * PASSAGE]
        bias_out[...] = folded


def attend_all(both_heads, id_table, count_table, pool_keys, pool_values, row_bias):
    seq_total, halves, rows_seq, _ = both_heads.shape
    pool_size = pool_keys.shape[0]
    width = pool_size * PASSAGE
    blocks_seq = rows_seq // BLOCK_LEN
    keys_flat = pool_keys.reshape(width, HEAD_DIM)
    values_flat = pool_values.reshape(width, HEAD_DIM)
    slot_index = jnp.arange(id_table.shape[1])
    picked = (slot_index[None, :] < count_table[:, None])[:, :, None] & (
        id_table[:, :, None] == jnp.arange(pool_size)[None, None, :]
    )
    usable = jnp.repeat(jnp.any(picked, axis=1).astype(jnp.float32), PASSAGE, axis=1)
    usable = usable.reshape(seq_total, blocks_seq, width)
    bias_wide = jnp.tile(row_bias[0], (1, pool_size))
    seqs_step = 2
    grid = (seq_total // seqs_step,)
    return pl.pallas_call(
        attend_kernel,
        grid=grid,
        in_specs=[
            pl.BlockSpec((seqs_step, halves, rows_seq, HEAD_DIM), lambda i: (i, 0, 0, 0)),
            pl.BlockSpec((width, HEAD_DIM), lambda i: (0, 0)),
            pl.BlockSpec((width, HEAD_DIM), lambda i: (0, 0)),
            pl.BlockSpec((BLOCK_LEN, width), lambda i: (0, 0)),
            pl.BlockSpec((seqs_step, blocks_seq, width), lambda i: (i, 0, 0)),
        ],
        out_specs=[
            pl.BlockSpec((seqs_step, halves, rows_seq, HEAD_DIM), lambda i: (i, 0, 0, 0)),
            pl.BlockSpec((width, HEAD_DIM), lambda i: (0, 0)),
            pl.BlockSpec((width, HEAD_DIM), lambda i: (0, 0)),
            pl.BlockSpec((BLOCK_LEN, PASSAGE), lambda i: (0, 0)),
        ],
        out_shape=[
            jax.ShapeDtypeStruct(both_heads.shape, jnp.bfloat16),
            jax.ShapeDtypeStruct((width, HEAD_DIM), jnp.bfloat16),
            jax.ShapeDtypeStruct((width, HEAD_DIM), jnp.bfloat16),
            jax.ShapeDtypeStruct((BLOCK_LEN, PASSAGE), jnp.float32),
        ],
        scratch_shapes=[
            pltpu.VMEM((width, HEAD_DIM), jnp.float32),
            pltpu.VMEM((width, HEAD_DIM), jnp.float32),
            pltpu.VMEM((BLOCK_LEN, width), jnp.float32),
        ],
        compiler_params=pltpu.CompilerParams(dimension_semantics=("arbitrary",)),
    )(both_heads, keys_flat, values_flat, bias_wide, usable)


def reduce_groups(part, mesh_shape):
    for axis in ("dp", "seq"):
        size = mesh_shape[axis]
        step = 1
        while step < size:
            pairs = [(index, index ^ step) for index in range(size)]
            part = part + lax.ppermute(part, axis, pairs)
            step *= 2
    return part


def local(mesh_shape, queries, cotangent, key_pool, value_pool, counts, neighbour_ids, rel_bias):
    token_rows = queries.shape[1]
    full_width = queries.shape[2]
    blocks_here = token_rows // BLOCK_LEN
    head_width = key_pool.shape[-1]
    heads_total = full_width // HEAD_DIM
    pool_size = key_pool.shape[2]
    pool_keys = key_pool.reshape(pool_size, PASSAGE, head_width)
    pool_values = value_pool.reshape(pool_size, PASSAGE, head_width)
    id_table = neighbour_ids.reshape(-1, neighbour_ids.shape[-1])
    count_table = counts.reshape(-1)
    row_bias = bias_rows(rel_bias)
    both_rows = jnp.stack(
        [
            queries.reshape(token_rows, heads_total, HEAD_DIM),
            cotangent.reshape(token_rows, heads_total, HEAD_DIM),
        ]
    ).transpose(2, 0, 1, 3)
    both_heads = lax.all_to_all(both_rows, "enc", split_axis=0, concat_axis=0, tiled=True)
    both_out, key_total, value_total, bias_total = attend_all(
        both_heads, id_table, count_table, pool_keys, pool_values, row_bias
    )
    both_back = lax.all_to_all(both_out, "enc", split_axis=0, concat_axis=0, tiled=True)
    both_back = both_back.transpose(1, 2, 0, 3).reshape((2,) + queries.shape)
    bias_grad = reduce_groups(fold_bias(bias_total[None], rel_bias.shape[1]), mesh_shape)
    return (
        both_back[0],
        both_back[1],
        key_total.reshape(key_pool.shape),
        value_total.reshape(value_pool.shape),
        bias_grad,
    )


def solution(mesh):
    in_specs = (
        P(("dp", "enc"), "seq", None),
        P(("dp", "enc"), "seq", None),
        P("dp", "seq", None, None, "enc"),
        P("dp", "seq", None, None, "enc"),
        P("dp", "seq"),
        P("dp", "seq", None),
        P("enc", None),
    )
    out_specs = (
        P(("dp", "enc"), "seq", None),
        P(("dp", "enc"), "seq", None),
        P("dp", "seq", None, None, "enc"),
        P("dp", "seq", None, None, "enc"),
        P("enc", None),
    )
    return jax.shard_map(functools.partial(local, dict(mesh.shape)), mesh=mesh, in_specs=in_specs, out_specs=out_specs, check_vma=False)
```

```python
import math

import jax
import jax.numpy as jnp
from jax import lax
from jax.experimental import pallas as pl
from jax.experimental.pallas import tpu as pltpu
from jax.sharding import PartitionSpec as P

HEAD_DIM = 128
BLOCK_LEN = 64
PASSAGE = 128


NEG_FILL = -1e30


def bias_rows(bias_table):
    heads_here, table_width = bias_table.shape
    padded = jnp.pad(bias_table, ((0, 0), (0, 1)))
    tiled_rows = jnp.broadcast_to(padded[:, None, :], (heads_here, BLOCK_LEN, table_width + 1))
    tiled_rows = tiled_rows.reshape(heads_here, BLOCK_LEN * (table_width + 1))[
        :, : BLOCK_LEN * table_width
    ]
    tiled_rows = tiled_rows.reshape(heads_here, BLOCK_LEN, table_width)
    return tiled_rows[:, :, BLOCK_LEN - 1 : BLOCK_LEN - 1 + PASSAGE]


def fold_bias(totals, table_width):
    heads_here = totals.shape[0]
    padded = jnp.pad(totals, ((0, 0), (0, 0), (BLOCK_LEN - 1, 0)))
    flat_rows = padded.reshape(heads_here, BLOCK_LEN * table_width)
    flat_rows = jnp.pad(flat_rows, ((0, 0), (0, BLOCK_LEN)))
    return flat_rows.reshape(heads_here, BLOCK_LEN, table_width + 1).sum(axis=1)[:, :table_width]


def attend_kernel(qd_ref, keys_ref, values_ref, bias_ref, mask_ref, out_ref, key_out, value_out,
                  bias_out, key_acc, value_acc, bias_acc):
    step = pl.program_id(0)
    score_scale = 1.0 / math.sqrt(HEAD_DIM)
    seqs_here, halves, rows_seq, _ = qd_ref.shape
    blocks_seq = rows_seq // BLOCK_LEN
    rows = seqs_here * rows_seq
    width = keys_ref.shape[0]
    tile4 = (seqs_here, blocks_seq, BLOCK_LEN, width)
    contract_last = (((1,), (1,)), ((), ()))
    contract_first = (((0,), (0,)), ((), ()))

    @pl.when(step == 0)
    def _():
        key_acc[...] = jnp.zeros_like(key_acc)
        value_acc[...] = jnp.zeros_like(value_acc)
        bias_acc[...] = jnp.zeros_like(bias_acc)

    query_rows = qd_ref[:, 0].reshape(rows, HEAD_DIM)
    grad_rows = qd_ref[:, 1].reshape(rows, HEAD_DIM)
    keys = keys_ref[...]
    values = values_ref[...]
    scores = lax.dot_general(query_rows, keys, contract_last, preferred_element_type=jnp.float32)
    scores = scores.reshape(tile4) * score_scale + bias_ref[...][None, None]
    usable = mask_ref[...][:, :, None, :] > 0.5
    masked = jnp.where(usable, scores, NEG_FILL)
    row_top = jnp.max(masked, axis=3, keepdims=True)
    raised = jnp.exp(masked - row_top)
    total = jnp.sum(raised, axis=3, keepdims=True)
    any_used = jnp.max(mask_ref[...], axis=2, keepdims=True)[:, :, :, None] > 0.5
    row_scale = jnp.where(any_used, 1.0 / total, 0.0)
    weights = raised * row_scale
    weights_low = weights.astype(jnp.bfloat16).reshape(rows, width)
    context = jnp.dot(weights_low, values, preferred_element_type=jnp.float32)
    grad_weights = lax.dot_general(grad_rows, values, contract_last, preferred_element_type=jnp.float32)
    grad_weights = grad_weights.reshape(tile4)
    row_delta = jnp.sum(weights * grad_weights, axis=3, keepdims=True)
    grad_scores = weights * (grad_weights - row_delta)
    scores_low = grad_scores.astype(jnp.bfloat16).reshape(rows, width)
    query_grad = score_scale * jnp.dot(scores_low, keys, preferred_element_type=jnp.float32)
    out_ref[:, 0] = context.astype(jnp.bfloat16).reshape(seqs_here, rows_seq, HEAD_DIM)
    out_ref[:, 1] = query_grad.astype(jnp.bfloat16).reshape(seqs_here, rows_seq, HEAD_DIM)
    key_acc[...] += lax.dot_general(scores_low, query_rows, contract_first, preferred_element_type=jnp.float32)
    value_acc[...] += lax.dot_general(weights_low, grad_rows, contract_first, preferred_element_type=jnp.float32)
    bias_acc[...] += jnp.sum(grad_scores, axis=(0, 1))

    @pl.when(step == pl.num_programs(0) - 1)
    def _():
        key_out[...] = (score_scale * key_acc[...]).astype(key_out.dtype)
        value_out[...] = value_acc[...].astype(value_out.dtype)
        folded = bias_acc[:, 0:PASSAGE]
        for part in range(1, width // PASSAGE):
            folded = folded + bias_acc[:, part * PASSAGE:(part + 1) * PASSAGE]
        bias_out[...] = folded


def attend_all(both_heads, id_table, count_table, pool_keys, pool_values, row_bias):
    seq_total, halves, rows_seq, _ = both_heads.shape
    pool_size = pool_keys.shape[0]
    width = pool_size * PASSAGE
    blocks_seq = rows_seq // BLOCK_LEN
    keys_flat = pool_keys.reshape(width, HEAD_DIM)
    values_flat = pool_values.reshape(width, HEAD_DIM)
    slot_index = jnp.arange(id_table.shape[1])
    picked = (slot_index[None, :] < count_table[:, None])[:, :, None] & (
        id_table[:, :, None] == jnp.arange(pool_size)[None, None, :]
    )
    usable = jnp.repeat(jnp.any(picked, axis=1).astype(jnp.float32), PASSAGE, axis=1)
    usable = usable.reshape(seq_total, blocks_seq, width)
    bias_wide = jnp.tile(row_bias[0], (1, pool_size))
    seqs_step = 2
    grid = (seq_total // seqs_step,)
    return pl.pallas_call(
        attend_kernel,
        grid=grid,
        in_specs=[
            pl.BlockSpec((seqs_step, halves, rows_seq, HEAD_DIM), lambda i: (i, 0, 0, 0)),
            pl.BlockSpec((width, HEAD_DIM), lambda i: (0, 0)),
            pl.BlockSpec((width, HEAD_DIM), lambda i: (0, 0)),
            pl.BlockSpec((BLOCK_LEN, width), lambda i: (0, 0)),
            pl.BlockSpec((seqs_step, blocks_seq, width), lambda i: (i, 0, 0)),
        ],
        out_specs=[
            pl.BlockSpec((seqs_step, halves, rows_seq, HEAD_DIM), lambda i: (i, 0, 0, 0)),
            pl.BlockSpec((width, HEAD_DIM), lambda i: (0, 0)),
            pl.BlockSpec((width, HEAD_DIM), lambda i: (0, 0)),
            pl.BlockSpec((BLOCK_LEN, PASSAGE), lambda i: (0, 0)),
        ],
        out_shape=[
            jax.ShapeDtypeStruct(both_heads.shape, jnp.bfloat16),
            jax.ShapeDtypeStruct((width, HEAD_DIM), jnp.bfloat16),
            jax.ShapeDtypeStruct((width, HEAD_DIM), jnp.bfloat16),
            jax.ShapeDtypeStruct((BLOCK_LEN, PASSAGE), jnp.float32),
        ],
        scratch_shapes=[
            pltpu.VMEM((width, HEAD_DIM), jnp.float32),
            pltpu.VMEM((width, HEAD_DIM), jnp.float32),
            pltpu.VMEM((BLOCK_LEN, width), jnp.float32),
        ],
        compiler_params=pltpu.CompilerParams(dimension_semantics=("arbitrary",)),
    )(both_heads, keys_flat, values_flat, bias_wide, usable)


def reduce_groups(part):
    return lax.psum(lax.psum(part, "dp"), "seq")


def local(queries, cotangent, key_pool, value_pool, counts, neighbour_ids, rel_bias):
    token_rows = queries.shape[1]
    full_width = queries.shape[2]
    blocks_here = token_rows // BLOCK_LEN
    head_width = key_pool.shape[-1]
    heads_total = full_width // HEAD_DIM
    pool_size = key_pool.shape[2]
    pool_keys = key_pool.reshape(pool_size, PASSAGE, head_width)
    pool_values = value_pool.reshape(pool_size, PASSAGE, head_width)
    id_table = neighbour_ids.reshape(-1, neighbour_ids.shape[-1])
    count_table = counts.reshape(-1)
    row_bias = bias_rows(rel_bias)
    both_rows = jnp.stack(
        [
            queries.reshape(token_rows, heads_total, HEAD_DIM),
            cotangent.reshape(token_rows, heads_total, HEAD_DIM),
        ]
    ).transpose(2, 0, 1, 3)
    both_heads = lax.all_to_all(both_rows, "enc", split_axis=0, concat_axis=0, tiled=True)
    both_out, key_total, value_total, bias_total = attend_all(
        both_heads, id_table, count_table, pool_keys, pool_values, row_bias
    )
    both_back = lax.all_to_all(both_out, "enc", split_axis=0, concat_axis=0, tiled=True)
    both_back = both_back.transpose(1, 2, 0, 3).reshape((2,) + queries.shape)
    bias_grad = reduce_groups(fold_bias(bias_total[None], rel_bias.shape[1]))
    return (
        both_back[0],
        both_back[1],
        key_total.reshape(key_pool.shape),
        value_total.reshape(value_pool.shape),
        bias_grad,
    )


def solution(mesh):
    in_specs = (
        P(("dp", "enc"), "seq", None),
        P(("dp", "enc"), "seq", None),
        P("dp", "seq", None, None, "enc"),
        P("dp", "seq", None, None, "enc"),
        P("dp", "seq"),
        P("dp", "seq", None),
        P("enc", None),
    )
    out_specs = (
        P(("dp", "enc"), "seq", None),
        P(("dp", "enc"), "seq", None),
        P("dp", "seq", None, None, "enc"),
        P("dp", "seq", None, None, "enc"),
        P("enc", None),
    )
    return jax.shard_map(local, mesh=mesh, in_specs=in_specs, out_specs=out_specs, check_vma=False)
```

```python
import math

import jax
import jax.numpy as jnp
from jax import lax
from jax.experimental import pallas as pl
from jax.experimental.pallas import tpu as pltpu
from jax.sharding import PartitionSpec as P

HEAD_DIM = 128
BLOCK_LEN = 64
PASSAGE = 128


NEG_FILL = -1e30


def bias_rows(bias_table):
    heads_here, table_width = bias_table.shape
    padded = jnp.pad(bias_table, ((0, 0), (0, 1)))
    tiled_rows = jnp.broadcast_to(padded[:, None, :], (heads_here, BLOCK_LEN, table_width + 1))
    tiled_rows = tiled_rows.reshape(heads_here, BLOCK_LEN * (table_width + 1))[
        :, : BLOCK_LEN * table_width
    ]
    tiled_rows = tiled_rows.reshape(heads_here, BLOCK_LEN, table_width)
    return tiled_rows[:, :, BLOCK_LEN - 1 : BLOCK_LEN - 1 + PASSAGE]


def fold_bias(totals, table_width):
    heads_here = totals.shape[0]
    padded = jnp.pad(totals, ((0, 0), (0, 0), (BLOCK_LEN - 1, 0)))
    flat_rows = padded.reshape(heads_here, BLOCK_LEN * table_width)
    flat_rows = jnp.pad(flat_rows, ((0, 0), (0, BLOCK_LEN)))
    return flat_rows.reshape(heads_here, BLOCK_LEN, table_width + 1).sum(axis=1)[:, :table_width]


def attend_kernel(qd_ref, keys_ref, values_ref, bias_ref, mask_ref, out_ref, key_out, value_out,
                  bias_out, key_acc, value_acc, bias_acc):
    step = pl.program_id(0)
    score_scale = 1.0 / math.sqrt(HEAD_DIM)
    seqs_here, halves, rows_seq, _ = qd_ref.shape
    blocks_seq = rows_seq // BLOCK_LEN
    rows = seqs_here * rows_seq
    width = keys_ref.shape[0]
    tile4 = (seqs_here, blocks_seq, BLOCK_LEN, width)
    contract_last = (((1,), (1,)), ((), ()))
    contract_first = (((0,), (0,)), ((), ()))

    @pl.when(step == 0)
    def _():
        key_acc[...] = jnp.zeros_like(key_acc)
        value_acc[...] = jnp.zeros_like(value_acc)
        bias_acc[...] = jnp.zeros_like(bias_acc)

    query_rows = qd_ref[:, 0].reshape(rows, HEAD_DIM)
    grad_rows = qd_ref[:, 1].reshape(rows, HEAD_DIM)
    keys = keys_ref[...]
    values = values_ref[...]
    scores = lax.dot_general(query_rows, keys, contract_last, preferred_element_type=jnp.float32)
    scores = scores.reshape(tile4) * score_scale + bias_ref[...][None, None]
    usable = mask_ref[...][:, :, None, :] > 0.5
    masked = jnp.where(usable, scores, NEG_FILL)
    row_top = jnp.max(masked, axis=3, keepdims=True)
    raised = jnp.exp(masked - row_top)
    total = jnp.sum(raised, axis=3, keepdims=True)
    any_used = jnp.max(mask_ref[...], axis=2, keepdims=True)[:, :, :, None] > 0.5
    row_scale = jnp.where(any_used, 1.0 / total, 0.0)
    weights = raised * row_scale
    weights_low = weights.astype(jnp.bfloat16).reshape(rows, width)
    context = jnp.dot(weights_low, values, preferred_element_type=jnp.float32)
    grad_weights = lax.dot_general(grad_rows, values, contract_last, preferred_element_type=jnp.float32)
    grad_weights = grad_weights.reshape(tile4)
    row_delta = jnp.sum(weights * grad_weights, axis=3, keepdims=True)
    grad_scores = weights * (grad_weights - row_delta)
    scores_low = grad_scores.astype(jnp.bfloat16).reshape(rows, width)
    query_grad = score_scale * jnp.dot(scores_low, keys, preferred_element_type=jnp.float32)
    out_ref[:, 0] = context.astype(jnp.bfloat16).reshape(seqs_here, rows_seq, HEAD_DIM)
    out_ref[:, 1] = query_grad.astype(jnp.bfloat16).reshape(seqs_here, rows_seq, HEAD_DIM)
    key_acc[...] += lax.dot_general(scores_low, query_rows, contract_first, preferred_element_type=jnp.float32)
    value_acc[...] += lax.dot_general(weights_low, grad_rows, contract_first, preferred_element_type=jnp.float32)
    bias_acc[...] += jnp.sum(grad_scores, axis=(0, 1))

    @pl.when(step == pl.num_programs(0) - 1)
    def _():
        key_out[...] = key_acc[...]
        value_out[...] = value_acc[...]
        folded = bias_acc[:, 0:PASSAGE]
        for part in range(1, width // PASSAGE):
            folded = folded + bias_acc[:, part * PASSAGE:(part + 1) * PASSAGE]
        bias_out[...] = folded


def attend_all(both_heads, usable, keys_flat, values_flat, bias_wide):
    seq_total, halves, rows_seq, _ = both_heads.shape
    width = keys_flat.shape[0]
    blocks_seq = rows_seq // BLOCK_LEN
    seqs_step = 2
    grid = (seq_total // seqs_step,)
    return pl.pallas_call(
        attend_kernel,
        grid=grid,
        in_specs=[
            pl.BlockSpec((seqs_step, halves, rows_seq, HEAD_DIM), lambda i: (i, 0, 0, 0)),
            pl.BlockSpec((width, HEAD_DIM), lambda i: (0, 0)),
            pl.BlockSpec((width, HEAD_DIM), lambda i: (0, 0)),
            pl.BlockSpec((BLOCK_LEN, width), lambda i: (0, 0)),
            pl.BlockSpec((seqs_step, blocks_seq, width), lambda i: (i, 0, 0)),
        ],
        out_specs=[
            pl.BlockSpec((seqs_step, halves, rows_seq, HEAD_DIM), lambda i: (i, 0, 0, 0)),
            pl.BlockSpec((width, HEAD_DIM), lambda i: (0, 0)),
            pl.BlockSpec((width, HEAD_DIM), lambda i: (0, 0)),
            pl.BlockSpec((BLOCK_LEN, PASSAGE), lambda i: (0, 0)),
        ],
        out_shape=[
            jax.ShapeDtypeStruct(both_heads.shape, jnp.bfloat16),
            jax.ShapeDtypeStruct((width, HEAD_DIM), jnp.float32),
            jax.ShapeDtypeStruct((width, HEAD_DIM), jnp.float32),
            jax.ShapeDtypeStruct((BLOCK_LEN, PASSAGE), jnp.float32),
        ],
        scratch_shapes=[
            pltpu.VMEM((width, HEAD_DIM), jnp.float32),
            pltpu.VMEM((width, HEAD_DIM), jnp.float32),
            pltpu.VMEM((BLOCK_LEN, width), jnp.float32),
        ],
        compiler_params=pltpu.CompilerParams(dimension_semantics=("arbitrary",)),
    )(both_heads, keys_flat, values_flat, bias_wide, usable)


def reduce_groups(part):
    return lax.psum(lax.psum(part, "dp"), "seq")


def local(queries, cotangent, key_pool, value_pool, counts, neighbour_ids, rel_bias):
    token_rows = queries.shape[1]
    full_width = queries.shape[2]
    blocks_here = token_rows // BLOCK_LEN
    head_width = key_pool.shape[-1]
    heads_total = full_width // HEAD_DIM
    pool_size = key_pool.shape[2]
    pool_keys = key_pool.reshape(pool_size, PASSAGE, head_width)
    pool_values = value_pool.reshape(pool_size, PASSAGE, head_width)
    id_table = neighbour_ids.reshape(-1, neighbour_ids.shape[-1])
    count_table = counts.reshape(-1)
    row_bias = bias_rows(rel_bias)
    score_scale = 1.0 / math.sqrt(HEAD_DIM)
    width = pool_size * PASSAGE
    keys_flat = pool_keys.reshape(width, HEAD_DIM)
    values_flat = pool_values.reshape(width, HEAD_DIM)
    slot_index = jnp.arange(id_table.shape[1])
    picked = (slot_index[None, :] < count_table[:, None])[:, :, None] & (
        id_table[:, :, None] == jnp.arange(pool_size)[None, None, :]
    )
    usable = jnp.repeat(jnp.any(picked, axis=1).astype(jnp.float32), PASSAGE, axis=1)
    usable = usable.reshape(-1, blocks_here, width)
    bias_wide = jnp.tile(row_bias[0], (1, pool_size))
    both_rows = jnp.stack(
        [
            queries.reshape(token_rows, heads_total, HEAD_DIM),
            cotangent.reshape(token_rows, heads_total, HEAD_DIM),
        ]
    ).transpose(2, 0, 1, 3)
    outs, key_parts, value_parts, bias_parts = [], [], [], []
    for block in range(blocks_here):
        chunk = both_rows[:, :, block * BLOCK_LEN:(block + 1) * BLOCK_LEN]
        chunk_heads = lax.all_to_all(chunk, "enc", split_axis=0, concat_axis=0, tiled=True)
        chunk_out, key_part, value_part, bias_part = attend_all(
            chunk_heads, usable[:, block:block + 1], keys_flat, values_flat, bias_wide
        )
        outs.append(lax.all_to_all(chunk_out, "enc", split_axis=0, concat_axis=0, tiled=True))
        key_parts.append(key_part)
        value_parts.append(value_part)
        bias_parts.append(bias_part)
    key_total = (score_scale * sum(key_parts[1:], key_parts[0])).astype(jnp.bfloat16)
    value_total = sum(value_parts[1:], value_parts[0]).astype(jnp.bfloat16)
    bias_total = sum(bias_parts[1:], bias_parts[0])
    both_back = jnp.concatenate(outs, axis=2)
    both_back = both_back.transpose(1, 2, 0, 3).reshape((2,) + queries.shape)
    bias_grad = reduce_groups(fold_bias(bias_total[None], rel_bias.shape[1]))
    return (
        both_back[0],
        both_back[1],
        key_total.reshape(key_pool.shape),
        value_total.reshape(value_pool.shape),
        bias_grad,
    )


def solution(mesh):
    in_specs = (
        P(("dp", "enc"), "seq", None),
        P(("dp", "enc"), "seq", None),
        P("dp", "seq", None, None, "enc"),
        P("dp", "seq", None, None, "enc"),
        P("dp", "seq"),
        P("dp", "seq", None),
        P("enc", None),
    )
    out_specs = (
        P(("dp", "enc"), "seq", None),
        P(("dp", "enc"), "seq", None),
        P("dp", "seq", None, None, "enc"),
        P("dp", "seq", None, None, "enc"),
        P("enc", None),
    )
    return jax.shard_map(local, mesh=mesh, in_specs=in_specs, out_specs=out_specs, check_vma=False)
```

```python
import math

import jax
import jax.numpy as jnp
from jax import lax
from jax.experimental import pallas as pl
from jax.experimental.pallas import tpu as pltpu
from jax.sharding import PartitionSpec as P

HEAD_DIM = 128
BLOCK_LEN = 64
PASSAGE = 128


NEG_FILL = -1e30


def bias_rows(bias_table):
    heads_here, table_width = bias_table.shape
    padded = jnp.pad(bias_table, ((0, 0), (0, 1)))
    tiled_rows = jnp.broadcast_to(padded[:, None, :], (heads_here, BLOCK_LEN, table_width + 1))
    tiled_rows = tiled_rows.reshape(heads_here, BLOCK_LEN * (table_width + 1))[
        :, : BLOCK_LEN * table_width
    ]
    tiled_rows = tiled_rows.reshape(heads_here, BLOCK_LEN, table_width)
    return tiled_rows[:, :, BLOCK_LEN - 1 : BLOCK_LEN - 1 + PASSAGE]


def fold_bias(totals, table_width):
    heads_here = totals.shape[0]
    padded = jnp.pad(totals, ((0, 0), (0, 0), (BLOCK_LEN - 1, 0)))
    flat_rows = padded.reshape(heads_here, BLOCK_LEN * table_width)
    flat_rows = jnp.pad(flat_rows, ((0, 0), (0, BLOCK_LEN)))
    return flat_rows.reshape(heads_here, BLOCK_LEN, table_width + 1).sum(axis=1)[:, :table_width]


def attend_kernel(qd_ref, keys_ref, values_ref, keys_t_ref, values_t_ref, bias_ref, mask_ref, out_ref, key_out, value_out,
                  bias_out, key_acc, value_acc, bias_acc):
    step = pl.program_id(0)
    score_scale = 1.0 / math.sqrt(HEAD_DIM)
    seqs_here, halves, rows_seq, _ = qd_ref.shape
    blocks_seq = rows_seq // BLOCK_LEN
    rows = seqs_here * rows_seq
    width = keys_t_ref.shape[1]
    tile4 = (seqs_here, blocks_seq, BLOCK_LEN, width)
    contract_first = (((0,), (0,)), ((), ()))

    @pl.when(step == 0)
    def _():
        key_acc[...] = jnp.zeros_like(key_acc)
        value_acc[...] = jnp.zeros_like(value_acc)
        bias_acc[...] = jnp.zeros_like(bias_acc)

    query_rows = qd_ref[:, 0].reshape(rows, HEAD_DIM)
    grad_rows = qd_ref[:, 1].reshape(rows, HEAD_DIM)
    keys = keys_ref[...]
    values = values_ref[...]
    scores = jnp.dot(query_rows, keys_t_ref[...], preferred_element_type=jnp.float32)
    scores = scores.reshape(tile4) * score_scale + bias_ref[...][None, None]
    usable = mask_ref[...][:, :, None, :] > 0.5
    masked = jnp.where(usable, scores, NEG_FILL)
    row_top = jnp.max(masked, axis=3, keepdims=True)
    raised = jnp.exp(masked - row_top)
    total = jnp.sum(raised, axis=3, keepdims=True)
    any_used = jnp.max(mask_ref[...], axis=2, keepdims=True)[:, :, :, None] > 0.5
    row_scale = jnp.where(any_used, 1.0 / total, 0.0)
    weights = raised * row_scale
    weights_low = weights.astype(jnp.bfloat16).reshape(rows, width)
    context = jnp.dot(weights_low, values, preferred_element_type=jnp.float32)
    grad_weights = jnp.dot(grad_rows, values_t_ref[...], preferred_element_type=jnp.float32)
    grad_weights = grad_weights.reshape(tile4)
    row_delta = jnp.sum(weights * grad_weights, axis=3, keepdims=True)
    grad_scores = weights * (grad_weights - row_delta)
    scores_low = grad_scores.astype(jnp.bfloat16).reshape(rows, width)
    query_grad = score_scale * jnp.dot(scores_low, keys, preferred_element_type=jnp.float32)
    out_ref[:, 0] = context.astype(jnp.bfloat16).reshape(seqs_here, rows_seq, HEAD_DIM)
    out_ref[:, 1] = query_grad.astype(jnp.bfloat16).reshape(seqs_here, rows_seq, HEAD_DIM)
    key_acc[...] += lax.dot_general(query_rows, scores_low, contract_first, preferred_element_type=jnp.float32)
    value_acc[...] += lax.dot_general(grad_rows, weights_low, contract_first, preferred_element_type=jnp.float32)
    bias_acc[...] += jnp.sum(grad_scores, axis=(0, 1))

    @pl.when(step == pl.num_programs(0) - 1)
    def _():
        key_out[...] = key_acc[...]
        value_out[...] = value_acc[...]
        folded = bias_acc[:, 0:PASSAGE]
        for part in range(1, width // PASSAGE):
            folded = folded + bias_acc[:, part * PASSAGE:(part + 1) * PASSAGE]
        bias_out[...] = folded


def attend_all(both_heads, id_table, count_table, pool_keys, pool_values, row_bias):
    seq_total, halves, rows_seq, _ = both_heads.shape
    pool_size = pool_keys.shape[0]
    width = pool_size * PASSAGE
    blocks_seq = rows_seq // BLOCK_LEN
    keys_flat = pool_keys.reshape(width, HEAD_DIM)
    values_flat = pool_values.reshape(width, HEAD_DIM)
    slot_index = jnp.arange(id_table.shape[1])
    picked = (slot_index[None, :] < count_table[:, None])[:, :, None] & (
        id_table[:, :, None] == jnp.arange(pool_size)[None, None, :]
    )
    usable = jnp.repeat(jnp.any(picked, axis=1).astype(jnp.float32), PASSAGE, axis=1)
    usable = usable.reshape(seq_total, blocks_seq, width)
    bias_wide = jnp.tile(row_bias[0], (1, pool_size))
    seqs_step = 4
    grid = (seq_total // seqs_step,)
    return pl.pallas_call(
        attend_kernel,
        grid=grid,
        in_specs=[
            pl.BlockSpec((seqs_step, halves, rows_seq, HEAD_DIM), lambda i: (i, 0, 0, 0)),
            pl.BlockSpec((width, HEAD_DIM), lambda i: (0, 0)),
            pl.BlockSpec((width, HEAD_DIM), lambda i: (0, 0)),
            pl.BlockSpec((HEAD_DIM, width), lambda i: (0, 0)),
            pl.BlockSpec((HEAD_DIM, width), lambda i: (0, 0)),
            pl.BlockSpec((BLOCK_LEN, width), lambda i: (0, 0)),
            pl.BlockSpec((seqs_step, blocks_seq, width), lambda i: (i, 0, 0)),
        ],
        out_specs=[
            pl.BlockSpec((seqs_step, halves, rows_seq, HEAD_DIM), lambda i: (i, 0, 0, 0)),
            pl.BlockSpec((HEAD_DIM, width), lambda i: (0, 0)),
            pl.BlockSpec((HEAD_DIM, width), lambda i: (0, 0)),
            pl.BlockSpec((BLOCK_LEN, PASSAGE), lambda i: (0, 0)),
        ],
        out_shape=[
            jax.ShapeDtypeStruct(both_heads.shape, jnp.bfloat16),
            jax.ShapeDtypeStruct((HEAD_DIM, width), jnp.float32),
            jax.ShapeDtypeStruct((HEAD_DIM, width), jnp.float32),
            jax.ShapeDtypeStruct((BLOCK_LEN, PASSAGE), jnp.float32),
        ],
        scratch_shapes=[
            pltpu.VMEM((HEAD_DIM, width), jnp.float32),
            pltpu.VMEM((HEAD_DIM, width), jnp.float32),
            pltpu.VMEM((BLOCK_LEN, width), jnp.float32),
        ],
        compiler_params=pltpu.CompilerParams(dimension_semantics=("arbitrary",)),
    )(both_heads, keys_flat, values_flat, keys_flat.T, values_flat.T, bias_wide, usable)


def reduce_groups(part):
    return lax.psum(lax.psum(part, "dp"), "seq")


def local(queries, cotangent, key_pool, value_pool, counts, neighbour_ids, rel_bias):
    token_rows = queries.shape[1]
    full_width = queries.shape[2]
    blocks_here = token_rows // BLOCK_LEN
    head_width = key_pool.shape[-1]
    heads_total = full_width // HEAD_DIM
    pool_size = key_pool.shape[2]
    pool_keys = key_pool.reshape(pool_size, PASSAGE, head_width)
    pool_values = value_pool.reshape(pool_size, PASSAGE, head_width)
    id_table = neighbour_ids.reshape(-1, neighbour_ids.shape[-1])
    count_table = counts.reshape(-1)
    row_bias = bias_rows(rel_bias)
    score_scale = 1.0 / math.sqrt(HEAD_DIM)
    both_rows = jnp.stack(
        [
            queries.reshape(token_rows, heads_total, HEAD_DIM),
            cotangent.reshape(token_rows, heads_total, HEAD_DIM),
        ]
    ).transpose(2, 0, 1, 3)
    both_heads = lax.all_to_all(both_rows, "enc", split_axis=0, concat_axis=0, tiled=True)
    both_out, key_total, value_total, bias_total = attend_all(
        both_heads, id_table, count_table, pool_keys, pool_values, row_bias
    )
    both_back = lax.all_to_all(both_out, "enc", split_axis=0, concat_axis=0, tiled=True)
    both_back = both_back.transpose(1, 2, 0, 3).reshape((2,) + queries.shape)
    bias_grad = reduce_groups(fold_bias(bias_total[None], rel_bias.shape[1]))
    return (
        both_back[0],
        both_back[1],
        (score_scale * key_total.T).astype(jnp.bfloat16).reshape(key_pool.shape),
        value_total.T.astype(jnp.bfloat16).reshape(value_pool.shape),
        bias_grad,
    )


def solution(mesh):
    in_specs = (
        P(("dp", "enc"), "seq", None),
        P(("dp", "enc"), "seq", None),
        P("dp", "seq", None, None, "enc"),
        P("dp", "seq", None, None, "enc"),
        P("dp", "seq"),
        P("dp", "seq", None),
        P("enc", None),
    )
    out_specs = (
        P(("dp", "enc"), "seq", None),
        P(("dp", "enc"), "seq", None),
        P("dp", "seq", None, None, "enc"),
        P("dp", "seq", None, None, "enc"),
        P("enc", None),
    )
    return jax.shard_map(local, mesh=mesh, in_specs=in_specs, out_specs=out_specs, check_vma=False)
```

```python
import math

import jax
import jax.numpy as jnp
from jax import lax
from jax.experimental import pallas as pl
from jax.experimental.pallas import tpu as pltpu
from jax.sharding import PartitionSpec as P

HEAD_DIM = 128
BLOCK_LEN = 64
PASSAGE = 128


NEG_FILL = -1e30


def bias_rows(bias_table):
    heads_here, table_width = bias_table.shape
    padded = jnp.pad(bias_table, ((0, 0), (0, 1)))
    tiled_rows = jnp.broadcast_to(padded[:, None, :], (heads_here, BLOCK_LEN, table_width + 1))
    tiled_rows = tiled_rows.reshape(heads_here, BLOCK_LEN * (table_width + 1))[
        :, : BLOCK_LEN * table_width
    ]
    tiled_rows = tiled_rows.reshape(heads_here, BLOCK_LEN, table_width)
    return tiled_rows[:, :, BLOCK_LEN - 1 : BLOCK_LEN - 1 + PASSAGE]


def fold_bias(totals, table_width):
    heads_here = totals.shape[0]
    padded = jnp.pad(totals, ((0, 0), (0, 0), (BLOCK_LEN - 1, 0)))
    flat_rows = padded.reshape(heads_here, BLOCK_LEN * table_width)
    flat_rows = jnp.pad(flat_rows, ((0, 0), (0, BLOCK_LEN)))
    return flat_rows.reshape(heads_here, BLOCK_LEN, table_width + 1).sum(axis=1)[:, :table_width]


def split_kernel(query_ref, grad_ref, out_ref):
    for head in range(out_ref.shape[0]):
        columns = slice(head * HEAD_DIM, (head + 1) * HEAD_DIM)
        out_ref[head, 0] = query_ref[:, columns]
        out_ref[head, 1] = grad_ref[:, columns]


def join_kernel(both_ref, context_ref, query_grad_ref):
    for head in range(both_ref.shape[0]):
        columns = slice(head * HEAD_DIM, (head + 1) * HEAD_DIM)
        context_ref[:, columns] = both_ref[head, 0]
        query_grad_ref[:, columns] = both_ref[head, 1]


def attend_kernel(qd_ref, keys_ref, values_ref, keys_t_ref, values_t_ref, bias_ref, mask_ref, out_ref, key_out, value_out,
                  bias_out, key_acc, value_acc, bias_acc):
    step = pl.program_id(0)
    score_scale = 1.0 / math.sqrt(HEAD_DIM)
    seqs_here, halves, rows_seq, _ = qd_ref.shape
    blocks_seq = rows_seq // BLOCK_LEN
    rows = seqs_here * rows_seq
    width = keys_t_ref.shape[1]
    tile4 = (seqs_here, blocks_seq, BLOCK_LEN, width)
    contract_first = (((0,), (0,)), ((), ()))

    @pl.when(step == 0)
    def _():
        key_acc[...] = jnp.zeros_like(key_acc)
        value_acc[...] = jnp.zeros_like(value_acc)
        bias_acc[...] = jnp.zeros_like(bias_acc)

    query_rows = qd_ref[:, 0].reshape(rows, HEAD_DIM)
    grad_rows = qd_ref[:, 1].reshape(rows, HEAD_DIM)
    keys = keys_ref[...]
    values = values_ref[...]
    scores = jnp.dot(query_rows, keys_t_ref[...], preferred_element_type=jnp.float32)
    scores = scores.reshape(tile4) * score_scale + bias_ref[...][None, None]
    usable = mask_ref[...][:, :, None, :] > 0.5
    masked = jnp.where(usable, scores, NEG_FILL)
    row_top = jnp.max(masked, axis=3, keepdims=True)
    raised = jnp.exp(masked - row_top)
    total = jnp.sum(raised, axis=3, keepdims=True)
    any_used = jnp.max(mask_ref[...], axis=2, keepdims=True)[:, :, :, None] > 0.5
    row_scale = jnp.where(any_used, 1.0 / total, 0.0)
    weights = raised * row_scale
    weights_low = weights.astype(jnp.bfloat16).reshape(rows, width)
    context = jnp.dot(weights_low, values, preferred_element_type=jnp.float32)
    grad_weights = jnp.dot(grad_rows, values_t_ref[...], preferred_element_type=jnp.float32)
    grad_weights = grad_weights.reshape(tile4)
    row_delta = jnp.sum(weights * grad_weights, axis=3, keepdims=True)
    grad_scores = weights * (grad_weights - row_delta)
    scores_low = grad_scores.astype(jnp.bfloat16).reshape(rows, width)
    query_grad = score_scale * jnp.dot(scores_low, keys, preferred_element_type=jnp.float32)
    out_ref[:, 0] = context.astype(jnp.bfloat16).reshape(seqs_here, rows_seq, HEAD_DIM)
    out_ref[:, 1] = query_grad.astype(jnp.bfloat16).reshape(seqs_here, rows_seq, HEAD_DIM)
    key_acc[...] += lax.dot_general(query_rows, scores_low, contract_first, preferred_element_type=jnp.float32)
    value_acc[...] += lax.dot_general(grad_rows, weights_low, contract_first, preferred_element_type=jnp.float32)
    bias_acc[...] += jnp.sum(grad_scores, axis=(0, 1))

    @pl.when(step == pl.num_programs(0) - 1)
    def _():
        key_out[...] = (score_scale * key_acc[...]).T.astype(key_out.dtype)
        value_out[...] = value_acc[...].T.astype(value_out.dtype)
        folded = bias_acc[:, 0:PASSAGE]
        for part in range(1, width // PASSAGE):
            folded = folded + bias_acc[:, part * PASSAGE:(part + 1) * PASSAGE]
        bias_out[...] = folded


def attend_all(both_heads, id_table, count_table, pool_keys, pool_values, row_bias):
    seq_total, halves, rows_seq, _ = both_heads.shape
    pool_size = pool_keys.shape[0]
    width = pool_size * PASSAGE
    blocks_seq = rows_seq // BLOCK_LEN
    keys_flat = pool_keys.reshape(width, HEAD_DIM)
    values_flat = pool_values.reshape(width, HEAD_DIM)
    slot_index = jnp.arange(id_table.shape[1])
    picked = (slot_index[None, :] < count_table[:, None])[:, :, None] & (
        id_table[:, :, None] == jnp.arange(pool_size)[None, None, :]
    )
    usable = jnp.repeat(jnp.any(picked, axis=1).astype(jnp.float32), PASSAGE, axis=1)
    usable = usable.reshape(seq_total, blocks_seq, width)
    bias_wide = jnp.tile(row_bias[0], (1, pool_size))
    seqs_step = 4
    grid = (seq_total // seqs_step,)
    return pl.pallas_call(
        attend_kernel,
        grid=grid,
        in_specs=[
            pl.BlockSpec((seqs_step, halves, rows_seq, HEAD_DIM), lambda i: (i, 0, 0, 0)),
            pl.BlockSpec((width, HEAD_DIM), lambda i: (0, 0)),
            pl.BlockSpec((width, HEAD_DIM), lambda i: (0, 0)),
            pl.BlockSpec((HEAD_DIM, width), lambda i: (0, 0)),
            pl.BlockSpec((HEAD_DIM, width), lambda i: (0, 0)),
            pl.BlockSpec((BLOCK_LEN, width), lambda i: (0, 0)),
            pl.BlockSpec((seqs_step, blocks_seq, width), lambda i: (i, 0, 0)),
        ],
        out_specs=[
            pl.BlockSpec((seqs_step, halves, rows_seq, HEAD_DIM), lambda i: (i, 0, 0, 0)),
            pl.BlockSpec((width, HEAD_DIM), lambda i: (0, 0)),
            pl.BlockSpec((width, HEAD_DIM), lambda i: (0, 0)),
            pl.BlockSpec((BLOCK_LEN, PASSAGE), lambda i: (0, 0)),
        ],
        out_shape=[
            jax.ShapeDtypeStruct(both_heads.shape, jnp.bfloat16),
            jax.ShapeDtypeStruct((width, HEAD_DIM), jnp.bfloat16),
            jax.ShapeDtypeStruct((width, HEAD_DIM), jnp.bfloat16),
            jax.ShapeDtypeStruct((BLOCK_LEN, PASSAGE), jnp.float32),
        ],
        scratch_shapes=[
            pltpu.VMEM((HEAD_DIM, width), jnp.float32),
            pltpu.VMEM((HEAD_DIM, width), jnp.float32),
            pltpu.VMEM((BLOCK_LEN, width), jnp.float32),
        ],
        compiler_params=pltpu.CompilerParams(dimension_semantics=("arbitrary",)),
    )(both_heads, keys_flat, values_flat, keys_flat.T, values_flat.T, bias_wide, usable)


def reduce_groups(part):
    return lax.psum(lax.psum(part, "dp"), "seq")


def local(queries, cotangent, key_pool, value_pool, counts, neighbour_ids, rel_bias):
    token_rows = queries.shape[1]
    full_width = queries.shape[2]
    blocks_here = token_rows // BLOCK_LEN
    head_width = key_pool.shape[-1]
    heads_total = full_width // HEAD_DIM
    pool_size = key_pool.shape[2]
    pool_keys = key_pool.reshape(pool_size, PASSAGE, head_width)
    pool_values = value_pool.reshape(pool_size, PASSAGE, head_width)
    id_table = neighbour_ids.reshape(-1, neighbour_ids.shape[-1])
    count_table = counts.reshape(-1)
    row_bias = bias_rows(rel_bias)
    score_scale = 1.0 / math.sqrt(HEAD_DIM)
    both_rows = pl.pallas_call(
        split_kernel,
        out_shape=jax.ShapeDtypeStruct((heads_total, 2, token_rows, HEAD_DIM), queries.dtype),
    )(queries.reshape(token_rows, full_width), cotangent.reshape(token_rows, full_width))
    both_heads = lax.all_to_all(both_rows, "enc", split_axis=0, concat_axis=0, tiled=True)
    both_out, key_total, value_total, bias_total = attend_all(
        both_heads, id_table, count_table, pool_keys, pool_values, row_bias
    )
    both_back = lax.all_to_all(both_out, "enc", split_axis=0, concat_axis=0, tiled=True)
    context_rows, query_rows_back = pl.pallas_call(
        join_kernel,
        out_shape=[jax.ShapeDtypeStruct((token_rows, full_width), queries.dtype)] * 2,
    )(both_back)
    bias_grad = reduce_groups(fold_bias(bias_total[None], rel_bias.shape[1]))
    return (
        context_rows.reshape(queries.shape),
        query_rows_back.reshape(queries.shape),
        key_total.reshape(key_pool.shape),
        value_total.reshape(value_pool.shape),
        bias_grad,
    )


def solution(mesh):
    in_specs = (
        P(("dp", "enc"), "seq", None),
        P(("dp", "enc"), "seq", None),
        P("dp", "seq", None, None, "enc"),
        P("dp", "seq", None, None, "enc"),
        P("dp", "seq"),
        P("dp", "seq", None),
        P("enc", None),
    )
    out_specs = (
        P(("dp", "enc"), "seq", None),
        P(("dp", "enc"), "seq", None),
        P("dp", "seq", None, None, "enc"),
        P("dp", "seq", None, None, "enc"),
        P("enc", None),
    )
    return jax.shard_map(local, mesh=mesh, in_specs=in_specs, out_specs=out_specs, check_vma=False)
```

```python
import math

import jax
import jax.numpy as jnp
from jax import lax
from jax.experimental import pallas as pl
from jax.experimental.pallas import tpu as pltpu
from jax.sharding import PartitionSpec as P

HEAD_DIM = 128
BLOCK_LEN = 64
PASSAGE = 128


NEG_FILL = -1e30


def bias_rows(bias_table):
    heads_here, table_width = bias_table.shape
    padded = jnp.pad(bias_table, ((0, 0), (0, 1)))
    tiled_rows = jnp.broadcast_to(padded[:, None, :], (heads_here, BLOCK_LEN, table_width + 1))
    tiled_rows = tiled_rows.reshape(heads_here, BLOCK_LEN * (table_width + 1))[
        :, : BLOCK_LEN * table_width
    ]
    tiled_rows = tiled_rows.reshape(heads_here, BLOCK_LEN, table_width)
    return tiled_rows[:, :, BLOCK_LEN - 1 : BLOCK_LEN - 1 + PASSAGE]


def fold_bias(totals, table_width):
    heads_here = totals.shape[0]
    padded = jnp.pad(totals, ((0, 0), (0, 0), (BLOCK_LEN - 1, 0)))
    flat_rows = padded.reshape(heads_here, BLOCK_LEN * table_width)
    flat_rows = jnp.pad(flat_rows, ((0, 0), (0, BLOCK_LEN)))
    return flat_rows.reshape(heads_here, BLOCK_LEN, table_width + 1).sum(axis=1)[:, :table_width]


def split_kernel(query_ref, grad_ref, out_ref):
    for head in range(out_ref.shape[0]):
        columns = slice(head * HEAD_DIM, (head + 1) * HEAD_DIM)
        out_ref[head, 0] = query_ref[:, columns]
        out_ref[head, 1] = grad_ref[:, columns]


def attend_kernel(qd_ref, keys_ref, values_ref, keys_t_ref, values_t_ref, bias_ref, mask_ref, out_ref, key_out, value_out,
                  bias_out, key_acc, value_acc, bias_acc):
    step = pl.program_id(0)
    score_scale = 1.0 / math.sqrt(HEAD_DIM)
    seqs_here, halves, rows_seq, _ = qd_ref.shape
    blocks_seq = rows_seq // BLOCK_LEN
    rows = seqs_here * rows_seq
    width = keys_t_ref.shape[1]
    tile4 = (seqs_here, blocks_seq, BLOCK_LEN, width)
    contract_first = (((0,), (0,)), ((), ()))

    @pl.when(step == 0)
    def _():
        key_acc[...] = jnp.zeros_like(key_acc)
        value_acc[...] = jnp.zeros_like(value_acc)
        bias_acc[...] = jnp.zeros_like(bias_acc)

    query_rows = qd_ref[:, 0].reshape(rows, HEAD_DIM)
    grad_rows = qd_ref[:, 1].reshape(rows, HEAD_DIM)
    keys = keys_ref[...]
    values = values_ref[...]
    scores = jnp.dot(query_rows, keys_t_ref[...], preferred_element_type=jnp.float32)
    scores = scores.reshape(tile4) * score_scale + bias_ref[...][None, None]
    usable = mask_ref[...][:, :, None, :] > 0.5
    masked = jnp.where(usable, scores, NEG_FILL)
    row_top = jnp.max(masked, axis=3, keepdims=True)
    raised = jnp.exp(masked - row_top)
    total = jnp.sum(raised, axis=3, keepdims=True)
    any_used = jnp.max(mask_ref[...], axis=2, keepdims=True)[:, :, :, None] > 0.5
    row_scale = jnp.where(any_used, 1.0 / total, 0.0)
    weights = raised * row_scale
    weights_low = weights.astype(jnp.bfloat16).reshape(rows, width)
    context = jnp.dot(weights_low, values, preferred_element_type=jnp.float32)
    grad_weights = jnp.dot(grad_rows, values_t_ref[...], preferred_element_type=jnp.float32)
    grad_weights = grad_weights.reshape(tile4)
    row_delta = jnp.sum(weights * grad_weights, axis=3, keepdims=True)
    grad_scores = weights * (grad_weights - row_delta)
    scores_low = grad_scores.astype(jnp.bfloat16).reshape(rows, width)
    query_grad = score_scale * jnp.dot(scores_low, keys, preferred_element_type=jnp.float32)
    out_ref[:, 0] = context.astype(jnp.bfloat16).reshape(seqs_here, rows_seq, HEAD_DIM)
    out_ref[:, 1] = query_grad.astype(jnp.bfloat16).reshape(seqs_here, rows_seq, HEAD_DIM)
    key_acc[...] += lax.dot_general(query_rows, scores_low, contract_first, preferred_element_type=jnp.float32)
    value_acc[...] += lax.dot_general(grad_rows, weights_low, contract_first, preferred_element_type=jnp.float32)
    bias_acc[...] += jnp.sum(grad_scores, axis=(0, 1))

    @pl.when(step == pl.num_programs(0) - 1)
    def _():
        key_out[...] = (score_scale * key_acc[...]).T.astype(key_out.dtype)
        value_out[...] = value_acc[...].T.astype(value_out.dtype)
        folded = bias_acc[:, 0:PASSAGE]
        for part in range(1, width // PASSAGE):
            folded = folded + bias_acc[:, part * PASSAGE:(part + 1) * PASSAGE]
        bias_out[...] = folded


def attend_all(both_heads, id_table, count_table, pool_keys, pool_values, row_bias):
    seq_total, halves, rows_seq, _ = both_heads.shape
    pool_size = pool_keys.shape[0]
    width = pool_size * PASSAGE
    blocks_seq = rows_seq // BLOCK_LEN
    keys_flat = pool_keys.reshape(width, HEAD_DIM)
    values_flat = pool_values.reshape(width, HEAD_DIM)
    slot_index = jnp.arange(id_table.shape[1])
    picked = (slot_index[None, :] < count_table[:, None])[:, :, None] & (
        id_table[:, :, None] == jnp.arange(pool_size)[None, None, :]
    )
    usable = jnp.repeat(jnp.any(picked, axis=1).astype(jnp.float32), PASSAGE, axis=1)
    usable = usable.reshape(seq_total, blocks_seq, width)
    bias_wide = jnp.tile(row_bias[0], (1, pool_size))
    seqs_step = 4
    grid = (seq_total // seqs_step,)
    return pl.pallas_call(
        attend_kernel,
        grid=grid,
        in_specs=[
            pl.BlockSpec((seqs_step, halves, rows_seq, HEAD_DIM), lambda i: (i, 0, 0, 0)),
            pl.BlockSpec((width, HEAD_DIM), lambda i: (0, 0)),
            pl.BlockSpec((width, HEAD_DIM), lambda i: (0, 0)),
            pl.BlockSpec((HEAD_DIM, width), lambda i: (0, 0)),
            pl.BlockSpec((HEAD_DIM, width), lambda i: (0, 0)),
            pl.BlockSpec((BLOCK_LEN, width), lambda i: (0, 0)),
            pl.BlockSpec((seqs_step, blocks_seq, width), lambda i: (i, 0, 0)),
        ],
        out_specs=[
            pl.BlockSpec((seqs_step, halves, rows_seq, HEAD_DIM), lambda i: (i, 0, 0, 0)),
            pl.BlockSpec((width, HEAD_DIM), lambda i: (0, 0)),
            pl.BlockSpec((width, HEAD_DIM), lambda i: (0, 0)),
            pl.BlockSpec((BLOCK_LEN, PASSAGE), lambda i: (0, 0)),
        ],
        out_shape=[
            jax.ShapeDtypeStruct(both_heads.shape, jnp.bfloat16),
            jax.ShapeDtypeStruct((width, HEAD_DIM), jnp.bfloat16),
            jax.ShapeDtypeStruct((width, HEAD_DIM), jnp.bfloat16),
            jax.ShapeDtypeStruct((BLOCK_LEN, PASSAGE), jnp.float32),
        ],
        scratch_shapes=[
            pltpu.VMEM((HEAD_DIM, width), jnp.float32),
            pltpu.VMEM((HEAD_DIM, width), jnp.float32),
            pltpu.VMEM((BLOCK_LEN, width), jnp.float32),
        ],
        compiler_params=pltpu.CompilerParams(dimension_semantics=("arbitrary",)),
    )(both_heads, keys_flat, values_flat, keys_flat.T, values_flat.T, bias_wide, usable)


def reduce_groups(part):
    return lax.psum(lax.psum(part, "dp"), "seq")


def local(queries, cotangent, key_pool, value_pool, counts, neighbour_ids, rel_bias):
    token_rows = queries.shape[1]
    full_width = queries.shape[2]
    blocks_here = token_rows // BLOCK_LEN
    head_width = key_pool.shape[-1]
    heads_total = full_width // HEAD_DIM
    pool_size = key_pool.shape[2]
    pool_keys = key_pool.reshape(pool_size, PASSAGE, head_width)
    pool_values = value_pool.reshape(pool_size, PASSAGE, head_width)
    id_table = neighbour_ids.reshape(-1, neighbour_ids.shape[-1])
    count_table = counts.reshape(-1)
    row_bias = bias_rows(rel_bias)
    score_scale = 1.0 / math.sqrt(HEAD_DIM)
    both_rows = pl.pallas_call(
        split_kernel,
        out_shape=jax.ShapeDtypeStruct((heads_total, 2, token_rows, HEAD_DIM), queries.dtype),
    )(queries.reshape(token_rows, full_width), cotangent.reshape(token_rows, full_width))
    both_heads = lax.all_to_all(both_rows, "enc", split_axis=0, concat_axis=0, tiled=True)
    both_out, key_total, value_total, bias_total = attend_all(
        both_heads, id_table, count_table, pool_keys, pool_values, row_bias
    )
    both_back = lax.all_to_all(both_out, "enc", split_axis=0, concat_axis=0, tiled=True)
    both_back = both_back.transpose(1, 2, 0, 3).reshape((2,) + queries.shape)
    bias_grad = reduce_groups(fold_bias(bias_total[None], rel_bias.shape[1]))
    return (
        both_back[0],
        both_back[1],
        key_total.reshape(key_pool.shape),
        value_total.reshape(value_pool.shape),
        bias_grad,
    )


def solution(mesh):
    in_specs = (
        P(("dp", "enc"), "seq", None),
        P(("dp", "enc"), "seq", None),
        P("dp", "seq", None, None, "enc"),
        P("dp", "seq", None, None, "enc"),
        P("dp", "seq"),
        P("dp", "seq", None),
        P("enc", None),
    )
    out_specs = (
        P(("dp", "enc"), "seq", None),
        P(("dp", "enc"), "seq", None),
        P("dp", "seq", None, None, "enc"),
        P("dp", "seq", None, None, "enc"),
        P("enc", None),
    )
    return jax.shard_map(local, mesh=mesh, in_specs=in_specs, out_specs=out_specs, check_vma=False)
```

```python
import math

import jax
import jax.numpy as jnp
from jax import lax
from jax.experimental import pallas as pl
from jax.experimental.pallas import tpu as pltpu
from jax.sharding import PartitionSpec as P

HEAD_DIM = 128
BLOCK_LEN = 64
PASSAGE = 128


NEG_FILL = -1e30


def bias_rows(bias_table):
    heads_here, table_width = bias_table.shape
    padded = jnp.pad(bias_table, ((0, 0), (0, 1)))
    tiled_rows = jnp.broadcast_to(padded[:, None, :], (heads_here, BLOCK_LEN, table_width + 1))
    tiled_rows = tiled_rows.reshape(heads_here, BLOCK_LEN * (table_width + 1))[
        :, : BLOCK_LEN * table_width
    ]
    tiled_rows = tiled_rows.reshape(heads_here, BLOCK_LEN, table_width)
    return tiled_rows[:, :, BLOCK_LEN - 1 : BLOCK_LEN - 1 + PASSAGE]


def fold_bias(totals, table_width):
    heads_here = totals.shape[0]
    padded = jnp.pad(totals, ((0, 0), (0, 0), (BLOCK_LEN - 1, 0)))
    flat_rows = padded.reshape(heads_here, BLOCK_LEN * table_width)
    flat_rows = jnp.pad(flat_rows, ((0, 0), (0, BLOCK_LEN)))
    return flat_rows.reshape(heads_here, BLOCK_LEN, table_width + 1).sum(axis=1)[:, :table_width]


def split_kernel(query_ref, grad_ref, out_ref):
    for head in range(out_ref.shape[0]):
        columns = slice(head * HEAD_DIM, (head + 1) * HEAD_DIM)
        out_ref[head, 0] = query_ref[:, columns]
        out_ref[head, 1] = grad_ref[:, columns]


def attend_kernel(qd_ref, keys_ref, values_ref, keys_t_ref, values_t_ref, bias_ref, mask_ref, out_ref, key_out, value_out,
                  bias_out, key_acc, value_acc, bias_acc):
    step = pl.program_id(0)
    score_scale = 1.0 / math.sqrt(HEAD_DIM)
    seqs_here, halves, rows_seq, _ = qd_ref.shape
    blocks_seq = rows_seq // BLOCK_LEN
    rows = seqs_here * rows_seq
    width = keys_t_ref.shape[1]
    tile4 = (seqs_here, blocks_seq, BLOCK_LEN, width)
    contract_first = (((0,), (0,)), ((), ()))

    @pl.when(step == 0)
    def _():
        key_acc[...] = jnp.zeros_like(key_acc)
        value_acc[...] = jnp.zeros_like(value_acc)
        bias_acc[...] = jnp.zeros_like(bias_acc)

    query_rows = qd_ref[:, 0].reshape(rows, HEAD_DIM)
    grad_rows = qd_ref[:, 1].reshape(rows, HEAD_DIM)
    keys = keys_ref[...]
    values = values_ref[...]
    scores = jnp.dot(query_rows, keys_t_ref[...], preferred_element_type=jnp.float32)
    scores = scores.reshape(tile4) * score_scale + bias_ref[...][None, None]
    usable = mask_ref[...][:, :, None, :] > 0.5
    masked = jnp.where(usable, scores, NEG_FILL)
    row_top = jnp.max(masked, axis=3, keepdims=True)
    raised = jnp.exp(masked - row_top)
    total = jnp.sum(raised, axis=3, keepdims=True)
    any_used = jnp.max(mask_ref[...], axis=2, keepdims=True)[:, :, :, None] > 0.5
    row_scale = jnp.where(any_used, 1.0 / total, 0.0)
    weights = raised * row_scale
    weights_low = weights.astype(jnp.bfloat16).reshape(rows, width)
    context = jnp.dot(weights_low, values, preferred_element_type=jnp.float32)
    grad_weights = jnp.dot(grad_rows, values_t_ref[...], preferred_element_type=jnp.float32)
    grad_weights = grad_weights.reshape(tile4)
    row_delta = jnp.sum(weights * grad_weights, axis=3, keepdims=True)
    grad_scores = weights * (grad_weights - row_delta)
    scores_low = grad_scores.astype(jnp.bfloat16).reshape(rows, width)
    query_grad = score_scale * jnp.dot(scores_low, keys, preferred_element_type=jnp.float32)
    out_ref[:, 0] = context.astype(jnp.bfloat16).reshape(seqs_here, rows_seq, HEAD_DIM)
    out_ref[:, 1] = query_grad.astype(jnp.bfloat16).reshape(seqs_here, rows_seq, HEAD_DIM)
    key_acc[...] += lax.dot_general(query_rows, scores_low, contract_first, preferred_element_type=jnp.float32)
    value_acc[...] += lax.dot_general(grad_rows, weights_low, contract_first, preferred_element_type=jnp.float32)
    bias_acc[...] += jnp.sum(grad_scores, axis=(0, 1))

    @pl.when(step == pl.num_programs(0) - 1)
    def _():
        key_out[...] = (score_scale * key_acc[...]).T.astype(key_out.dtype)
        value_out[...] = value_acc[...].T.astype(value_out.dtype)
        folded = bias_acc[:, 0:PASSAGE]
        for part in range(1, width // PASSAGE):
            folded = folded + bias_acc[:, part * PASSAGE:(part + 1) * PASSAGE]
        bias_out[...] = folded


def attend_all(both_heads, id_table, count_table, pool_keys, pool_values, row_bias):
    seq_total, halves, rows_seq, _ = both_heads.shape
    pool_size = pool_keys.shape[0]
    width = pool_size * PASSAGE
    blocks_seq = rows_seq // BLOCK_LEN
    keys_flat = pool_keys.reshape(width, HEAD_DIM)
    values_flat = pool_values.reshape(width, HEAD_DIM)
    slot_index = jnp.arange(id_table.shape[1])
    picked = (slot_index[None, :] < count_table[:, None])[:, :, None] & (
        id_table[:, :, None] == jnp.arange(pool_size)[None, None, :]
    )
    usable = jnp.repeat(jnp.any(picked, axis=1).astype(jnp.float32), PASSAGE, axis=1)
    usable = usable.reshape(seq_total, blocks_seq, width)
    bias_wide = jnp.tile(row_bias[0], (1, pool_size))
    seqs_step = 4
    grid = (seq_total // seqs_step,)
    return pl.pallas_call(
        attend_kernel,
        grid=grid,
        in_specs=[
            pl.BlockSpec((seqs_step, halves, rows_seq, HEAD_DIM), lambda i: (i, 0, 0, 0)),
            pl.BlockSpec((width, HEAD_DIM), lambda i: (0, 0)),
            pl.BlockSpec((width, HEAD_DIM), lambda i: (0, 0)),
            pl.BlockSpec((HEAD_DIM, width), lambda i: (0, 0)),
            pl.BlockSpec((HEAD_DIM, width), lambda i: (0, 0)),
            pl.BlockSpec((BLOCK_LEN, width), lambda i: (0, 0)),
            pl.BlockSpec((seqs_step, blocks_seq, width), lambda i: (i, 0, 0)),
        ],
        out_specs=[
            pl.BlockSpec((seqs_step, halves, rows_seq, HEAD_DIM), lambda i: (i, 0, 0, 0)),
            pl.BlockSpec((width, HEAD_DIM), lambda i: (0, 0)),
            pl.BlockSpec((width, HEAD_DIM), lambda i: (0, 0)),
            pl.BlockSpec((BLOCK_LEN, PASSAGE), lambda i: (0, 0)),
        ],
        out_shape=[
            jax.ShapeDtypeStruct(both_heads.shape, jnp.bfloat16),
            jax.ShapeDtypeStruct((width, HEAD_DIM), jnp.bfloat16),
            jax.ShapeDtypeStruct((width, HEAD_DIM), jnp.bfloat16),
            jax.ShapeDtypeStruct((BLOCK_LEN, PASSAGE), jnp.float32),
        ],
        scratch_shapes=[
            pltpu.VMEM((HEAD_DIM, width), jnp.float32),
            pltpu.VMEM((HEAD_DIM, width), jnp.float32),
            pltpu.VMEM((BLOCK_LEN, width), jnp.float32),
        ],
        compiler_params=pltpu.CompilerParams(dimension_semantics=("arbitrary",)),
    )(both_heads, keys_flat, values_flat, keys_flat.T, values_flat.T, bias_wide, usable)


def reduce_groups(part):
    return lax.psum(lax.psum(part, "seq"), "dp")


def local(queries, cotangent, key_pool, value_pool, counts, neighbour_ids, rel_bias):
    token_rows = queries.shape[1]
    full_width = queries.shape[2]
    blocks_here = token_rows // BLOCK_LEN
    head_width = key_pool.shape[-1]
    heads_total = full_width // HEAD_DIM
    pool_size = key_pool.shape[2]
    pool_keys = key_pool.reshape(pool_size, PASSAGE, head_width)
    pool_values = value_pool.reshape(pool_size, PASSAGE, head_width)
    id_table = neighbour_ids.reshape(-1, neighbour_ids.shape[-1])
    count_table = counts.reshape(-1)
    row_bias = bias_rows(rel_bias)
    score_scale = 1.0 / math.sqrt(HEAD_DIM)
    both_rows = pl.pallas_call(
        split_kernel,
        out_shape=jax.ShapeDtypeStruct((heads_total, 2, token_rows, HEAD_DIM), queries.dtype),
    )(queries.reshape(token_rows, full_width), cotangent.reshape(token_rows, full_width))
    both_heads = lax.all_to_all(both_rows, "enc", split_axis=0, concat_axis=0, tiled=True)
    both_out, key_total, value_total, bias_total = attend_all(
        both_heads, id_table, count_table, pool_keys, pool_values, row_bias
    )
    both_back = lax.all_to_all(both_out, "enc", split_axis=0, concat_axis=0, tiled=True)
    both_back = both_back.transpose(1, 2, 0, 3).reshape((2,) + queries.shape)
    bias_grad = reduce_groups(fold_bias(bias_total[None], rel_bias.shape[1]))
    return (
        both_back[0],
        both_back[1],
        key_total.reshape(key_pool.shape),
        value_total.reshape(value_pool.shape),
        bias_grad,
    )


def solution(mesh):
    in_specs = (
        P(("dp", "enc"), "seq", None),
        P(("dp", "enc"), "seq", None),
        P("dp", "seq", None, None, "enc"),
        P("dp", "seq", None, None, "enc"),
        P("dp", "seq"),
        P("dp", "seq", None),
        P("enc", None),
    )
    out_specs = (
        P(("dp", "enc"), "seq", None),
        P(("dp", "enc"), "seq", None),
        P("dp", "seq", None, None, "enc"),
        P("dp", "seq", None, None, "enc"),
        P("enc", None),
    )
    return jax.shard_map(local, mesh=mesh, in_specs=in_specs, out_specs=out_specs, check_vma=False)
```

```python
import math

import jax
import jax.numpy as jnp
from jax import lax
from jax.experimental import pallas as pl
from jax.experimental.pallas import tpu as pltpu
from jax.sharding import PartitionSpec as P

HEAD_DIM = 128
BLOCK_LEN = 64
PASSAGE = 128


NEG_FILL = -1e30


def bias_rows(bias_table):
    heads_here, table_width = bias_table.shape
    padded = jnp.pad(bias_table, ((0, 0), (0, 1)))
    tiled_rows = jnp.broadcast_to(padded[:, None, :], (heads_here, BLOCK_LEN, table_width + 1))
    tiled_rows = tiled_rows.reshape(heads_here, BLOCK_LEN * (table_width + 1))[
        :, : BLOCK_LEN * table_width
    ]
    tiled_rows = tiled_rows.reshape(heads_here, BLOCK_LEN, table_width)
    return tiled_rows[:, :, BLOCK_LEN - 1 : BLOCK_LEN - 1 + PASSAGE]


def fold_bias(totals, table_width):
    heads_here = totals.shape[0]
    padded = jnp.pad(totals, ((0, 0), (0, 0), (BLOCK_LEN - 1, 0)))
    flat_rows = padded.reshape(heads_here, BLOCK_LEN * table_width)
    flat_rows = jnp.pad(flat_rows, ((0, 0), (0, BLOCK_LEN)))
    return flat_rows.reshape(heads_here, BLOCK_LEN, table_width + 1).sum(axis=1)[:, :table_width]


def split_kernel(query_ref, grad_ref, out_ref):
    for head in range(out_ref.shape[0]):
        columns = slice(head * HEAD_DIM, (head + 1) * HEAD_DIM)
        out_ref[head, 0] = query_ref[:, columns]
        out_ref[head, 1] = grad_ref[:, columns]


def attend_kernel(qd_ref, keys_ref, values_ref, keys_t_ref, values_t_ref, bias_ref, mask_ref, out_ref, key_out, value_out,
                  bias_out, key_acc, value_acc, bias_acc):
    step = pl.program_id(0)
    score_scale = 1.0 / math.sqrt(HEAD_DIM)
    seqs_here, halves, rows_seq, _ = qd_ref.shape
    blocks_seq = rows_seq // BLOCK_LEN
    rows = seqs_here * rows_seq
    width = keys_t_ref.shape[1]
    tile4 = (seqs_here, blocks_seq, BLOCK_LEN, width)
    contract_first = (((0,), (0,)), ((), ()))

    @pl.when(step == 0)
    def _():
        key_acc[...] = jnp.zeros_like(key_acc)
        value_acc[...] = jnp.zeros_like(value_acc)
        bias_acc[...] = jnp.zeros_like(bias_acc)

    query_rows = qd_ref[:, 0].reshape(rows, HEAD_DIM)
    grad_rows = qd_ref[:, 1].reshape(rows, HEAD_DIM)
    keys = keys_ref[...]
    values = values_ref[...]
    scores = jnp.dot(query_rows, keys_t_ref[...], preferred_element_type=jnp.float32)
    scores = scores.reshape(tile4) * score_scale + bias_ref[...][None, None]
    usable = mask_ref[...][:, :, None, :] > 0.5
    masked = jnp.where(usable, scores, NEG_FILL)
    row_top = jnp.max(masked, axis=3, keepdims=True)
    raised = jnp.exp(masked - row_top)
    total = jnp.sum(raised, axis=3, keepdims=True)
    any_used = jnp.max(mask_ref[...], axis=2, keepdims=True)[:, :, :, None] > 0.5
    row_scale = jnp.where(any_used, 1.0 / total, 0.0)
    weights = raised * row_scale
    weights_low = weights.astype(jnp.bfloat16).reshape(rows, width)
    context = jnp.dot(weights_low, values, preferred_element_type=jnp.float32)
    grad_weights = jnp.dot(grad_rows, values_t_ref[...], preferred_element_type=jnp.float32)
    grad_weights = grad_weights.reshape(tile4)
    row_delta = jnp.sum(weights * grad_weights, axis=3, keepdims=True)
    grad_scores = weights * (grad_weights - row_delta)
    scores_low = grad_scores.astype(jnp.bfloat16).reshape(rows, width)
    query_grad = score_scale * jnp.dot(scores_low, keys, preferred_element_type=jnp.float32)
    out_ref[:, 0] = context.astype(jnp.bfloat16).reshape(seqs_here, rows_seq, HEAD_DIM)
    out_ref[:, 1] = query_grad.astype(jnp.bfloat16).reshape(seqs_here, rows_seq, HEAD_DIM)
    key_acc[...] += lax.dot_general(query_rows, scores_low, contract_first, preferred_element_type=jnp.float32)
    value_acc[...] += lax.dot_general(grad_rows, weights_low, contract_first, preferred_element_type=jnp.float32)
    bias_acc[...] += jnp.sum(grad_scores, axis=(0, 1))

    @pl.when(step == pl.num_programs(0) - 1)
    def _():
        key_out[...] = (score_scale * key_acc[...]).T.astype(key_out.dtype)
        value_out[...] = value_acc[...].T.astype(value_out.dtype)
        folded = bias_acc[:, 0:PASSAGE]
        for part in range(1, width // PASSAGE):
            folded = folded + bias_acc[:, part * PASSAGE:(part + 1) * PASSAGE]
        bias_out[...] = folded


def attend_all(both_heads, id_table, count_table, pool_keys, pool_values, row_bias):
    seq_total, halves, rows_seq, _ = both_heads.shape
    pool_size = pool_keys.shape[0]
    width = pool_size * PASSAGE
    blocks_seq = rows_seq // BLOCK_LEN
    keys_flat = pool_keys.reshape(width, HEAD_DIM)
    values_flat = pool_values.reshape(width, HEAD_DIM)
    slot_index = jnp.arange(id_table.shape[1])
    picked = (slot_index[None, :] < count_table[:, None])[:, :, None] & (
        id_table[:, :, None] == jnp.arange(pool_size)[None, None, :]
    )
    usable = jnp.repeat(jnp.any(picked, axis=1).astype(jnp.float32), PASSAGE, axis=1)
    usable = usable.reshape(seq_total, blocks_seq, width)
    bias_wide = jnp.tile(row_bias[0], (1, pool_size))
    seqs_step = 8
    grid = (seq_total // seqs_step,)
    return pl.pallas_call(
        attend_kernel,
        grid=grid,
        in_specs=[
            pl.BlockSpec((seqs_step, halves, rows_seq, HEAD_DIM), lambda i: (i, 0, 0, 0)),
            pl.BlockSpec((width, HEAD_DIM), lambda i: (0, 0)),
            pl.BlockSpec((width, HEAD_DIM), lambda i: (0, 0)),
            pl.BlockSpec((HEAD_DIM, width), lambda i: (0, 0)),
            pl.BlockSpec((HEAD_DIM, width), lambda i: (0, 0)),
            pl.BlockSpec((BLOCK_LEN, width), lambda i: (0, 0)),
            pl.BlockSpec((seqs_step, blocks_seq, width), lambda i: (i, 0, 0)),
        ],
        out_specs=[
            pl.BlockSpec((seqs_step, halves, rows_seq, HEAD_DIM), lambda i: (i, 0, 0, 0)),
            pl.BlockSpec((width, HEAD_DIM), lambda i: (0, 0)),
            pl.BlockSpec((width, HEAD_DIM), lambda i: (0, 0)),
            pl.BlockSpec((BLOCK_LEN, PASSAGE), lambda i: (0, 0)),
        ],
        out_shape=[
            jax.ShapeDtypeStruct(both_heads.shape, jnp.bfloat16),
            jax.ShapeDtypeStruct((width, HEAD_DIM), jnp.bfloat16),
            jax.ShapeDtypeStruct((width, HEAD_DIM), jnp.bfloat16),
            jax.ShapeDtypeStruct((BLOCK_LEN, PASSAGE), jnp.float32),
        ],
        scratch_shapes=[
            pltpu.VMEM((HEAD_DIM, width), jnp.float32),
            pltpu.VMEM((HEAD_DIM, width), jnp.float32),
            pltpu.VMEM((BLOCK_LEN, width), jnp.float32),
        ],
        compiler_params=pltpu.CompilerParams(dimension_semantics=("arbitrary",)),
    )(both_heads, keys_flat, values_flat, keys_flat.T, values_flat.T, bias_wide, usable)


def reduce_groups(part):
    return lax.psum(lax.psum(part, "seq"), "dp")


def local(queries, cotangent, key_pool, value_pool, counts, neighbour_ids, rel_bias):
    token_rows = queries.shape[1]
    full_width = queries.shape[2]
    blocks_here = token_rows // BLOCK_LEN
    head_width = key_pool.shape[-1]
    heads_total = full_width // HEAD_DIM
    pool_size = key_pool.shape[2]
    pool_keys = key_pool.reshape(pool_size, PASSAGE, head_width)
    pool_values = value_pool.reshape(pool_size, PASSAGE, head_width)
    id_table = neighbour_ids.reshape(-1, neighbour_ids.shape[-1])
    count_table = counts.reshape(-1)
    row_bias = bias_rows(rel_bias)
    score_scale = 1.0 / math.sqrt(HEAD_DIM)
    both_rows = pl.pallas_call(
        split_kernel,
        out_shape=jax.ShapeDtypeStruct((heads_total, 2, token_rows, HEAD_DIM), queries.dtype),
    )(queries.reshape(token_rows, full_width), cotangent.reshape(token_rows, full_width))
    both_heads = lax.all_to_all(both_rows, "enc", split_axis=0, concat_axis=0, tiled=True)
    both_out, key_total, value_total, bias_total = attend_all(
        both_heads, id_table, count_table, pool_keys, pool_values, row_bias
    )
    both_back = lax.all_to_all(both_out, "enc", split_axis=0, concat_axis=0, tiled=True)
    both_back = both_back.transpose(1, 2, 0, 3).reshape((2,) + queries.shape)
    bias_grad = reduce_groups(fold_bias(bias_total[None], rel_bias.shape[1]))
    return (
        both_back[0],
        both_back[1],
        key_total.reshape(key_pool.shape),
        value_total.reshape(value_pool.shape),
        bias_grad,
    )


def solution(mesh):
    in_specs = (
        P(("dp", "enc"), "seq", None),
        P(("dp", "enc"), "seq", None),
        P("dp", "seq", None, None, "enc"),
        P("dp", "seq", None, None, "enc"),
        P("dp", "seq"),
        P("dp", "seq", None),
        P("enc", None),
    )
    out_specs = (
        P(("dp", "enc"), "seq", None),
        P(("dp", "enc"), "seq", None),
        P("dp", "seq", None, None, "enc"),
        P("dp", "seq", None, None, "enc"),
        P("enc", None),
    )
    return jax.shard_map(local, mesh=mesh, in_specs=in_specs, out_specs=out_specs, check_vma=False)
```

```python
import math

import jax
import jax.numpy as jnp
from jax import lax
from jax.experimental import pallas as pl
from jax.experimental.pallas import tpu as pltpu
from jax.sharding import PartitionSpec as P

HEAD_DIM = 128
BLOCK_LEN = 64
PASSAGE = 128


NEG_FILL = -1e30


def bias_rows(bias_table):
    heads_here, table_width = bias_table.shape
    padded = jnp.pad(bias_table, ((0, 0), (0, 1)))
    tiled_rows = jnp.broadcast_to(padded[:, None, :], (heads_here, BLOCK_LEN, table_width + 1))
    tiled_rows = tiled_rows.reshape(heads_here, BLOCK_LEN * (table_width + 1))[
        :, : BLOCK_LEN * table_width
    ]
    tiled_rows = tiled_rows.reshape(heads_here, BLOCK_LEN, table_width)
    return tiled_rows[:, :, BLOCK_LEN - 1 : BLOCK_LEN - 1 + PASSAGE]


def fold_bias(totals, table_width):
    heads_here = totals.shape[0]
    padded = jnp.pad(totals, ((0, 0), (0, 0), (BLOCK_LEN - 1, 0)))
    flat_rows = padded.reshape(heads_here, BLOCK_LEN * table_width)
    flat_rows = jnp.pad(flat_rows, ((0, 0), (0, BLOCK_LEN)))
    return flat_rows.reshape(heads_here, BLOCK_LEN, table_width + 1).sum(axis=1)[:, :table_width]


def split_kernel(query_ref, grad_ref, out_ref, copy_sems):
    copies = []
    for head in range(out_ref.shape[0]):
        columns = pl.ds(head * HEAD_DIM, HEAD_DIM)
        for half, source in enumerate((query_ref, grad_ref)):
            copy = pltpu.make_async_copy(
                source.at[:, columns], out_ref.at[head, half], copy_sems.at[head, half]
            )
            copy.start()
            copies.append(copy)
    for copy in copies:
        copy.wait()


def attend_kernel(qd_ref, keys_ref, values_ref, keys_t_ref, values_t_ref, bias_ref, mask_ref, out_ref, key_out, value_out,
                  bias_out, key_acc, value_acc, bias_acc):
    step = pl.program_id(0)
    score_scale = 1.0 / math.sqrt(HEAD_DIM)
    seqs_here, halves, rows_seq, _ = qd_ref.shape
    blocks_seq = rows_seq // BLOCK_LEN
    rows = seqs_here * rows_seq
    width = keys_t_ref.shape[1]
    tile4 = (seqs_here, blocks_seq, BLOCK_LEN, width)
    contract_first = (((0,), (0,)), ((), ()))

    @pl.when(step == 0)
    def _():
        key_acc[...] = jnp.zeros_like(key_acc)
        value_acc[...] = jnp.zeros_like(value_acc)
        bias_acc[...] = jnp.zeros_like(bias_acc)

    query_rows = qd_ref[:, 0].reshape(rows, HEAD_DIM)
    grad_rows = qd_ref[:, 1].reshape(rows, HEAD_DIM)
    keys = keys_ref[...]
    values = values_ref[...]
    scores = jnp.dot(query_rows, keys_t_ref[...], preferred_element_type=jnp.float32)
    scores = scores.reshape(tile4) * score_scale + bias_ref[...][None, None]
    usable = mask_ref[...][:, :, None, :] > 0.5
    masked = jnp.where(usable, scores, NEG_FILL)
    row_top = jnp.max(masked, axis=3, keepdims=True)
    raised = jnp.exp(masked - row_top)
    total = jnp.sum(raised, axis=3, keepdims=True)
    any_used = jnp.max(mask_ref[...], axis=2, keepdims=True)[:, :, :, None] > 0.5
    row_scale = jnp.where(any_used, 1.0 / total, 0.0)
    weights = raised * row_scale
    weights_low = weights.astype(jnp.bfloat16).reshape(rows, width)
    context = jnp.dot(weights_low, values, preferred_element_type=jnp.float32)
    grad_weights = jnp.dot(grad_rows, values_t_ref[...], preferred_element_type=jnp.float32)
    grad_weights = grad_weights.reshape(tile4)
    row_delta = jnp.sum(weights * grad_weights, axis=3, keepdims=True)
    grad_scores = weights * (grad_weights - row_delta)
    scores_low = grad_scores.astype(jnp.bfloat16).reshape(rows, width)
    query_grad = score_scale * jnp.dot(scores_low, keys, preferred_element_type=jnp.float32)
    out_ref[:, 0] = context.astype(jnp.bfloat16).reshape(seqs_here, rows_seq, HEAD_DIM)
    out_ref[:, 1] = query_grad.astype(jnp.bfloat16).reshape(seqs_here, rows_seq, HEAD_DIM)
    key_acc[...] += lax.dot_general(query_rows, scores_low, contract_first, preferred_element_type=jnp.float32)
    value_acc[...] += lax.dot_general(grad_rows, weights_low, contract_first, preferred_element_type=jnp.float32)
    bias_acc[...] += jnp.sum(grad_scores, axis=(0, 1))

    @pl.when(step == pl.num_programs(0) - 1)
    def _():
        key_out[...] = (score_scale * key_acc[...]).T.astype(key_out.dtype)
        value_out[...] = value_acc[...].T.astype(value_out.dtype)
        folded = bias_acc[:, 0:PASSAGE]
        for part in range(1, width // PASSAGE):
            folded = folded + bias_acc[:, part * PASSAGE:(part + 1) * PASSAGE]
        bias_out[...] = folded


def attend_all(both_heads, id_table, count_table, pool_keys, pool_values, row_bias):
    seq_total, halves, rows_seq, _ = both_heads.shape
    pool_size = pool_keys.shape[0]
    width = pool_size * PASSAGE
    blocks_seq = rows_seq // BLOCK_LEN
    keys_flat = pool_keys.reshape(width, HEAD_DIM)
    values_flat = pool_values.reshape(width, HEAD_DIM)
    slot_index = jnp.arange(id_table.shape[1])
    picked = (slot_index[None, :] < count_table[:, None])[:, :, None] & (
        id_table[:, :, None] == jnp.arange(pool_size)[None, None, :]
    )
    usable = jnp.repeat(jnp.any(picked, axis=1).astype(jnp.float32), PASSAGE, axis=1)
    usable = usable.reshape(seq_total, blocks_seq, width)
    bias_wide = jnp.tile(row_bias[0], (1, pool_size))
    seqs_step = 8
    grid = (seq_total // seqs_step,)
    return pl.pallas_call(
        attend_kernel,
        grid=grid,
        in_specs=[
            pl.BlockSpec((seqs_step, halves, rows_seq, HEAD_DIM), lambda i: (i, 0, 0, 0)),
            pl.BlockSpec((width, HEAD_DIM), lambda i: (0, 0)),
            pl.BlockSpec((width, HEAD_DIM), lambda i: (0, 0)),
            pl.BlockSpec((HEAD_DIM, width), lambda i: (0, 0)),
            pl.BlockSpec((HEAD_DIM, width), lambda i: (0, 0)),
            pl.BlockSpec((BLOCK_LEN, width), lambda i: (0, 0)),
            pl.BlockSpec((seqs_step, blocks_seq, width), lambda i: (i, 0, 0)),
        ],
        out_specs=[
            pl.BlockSpec((seqs_step, halves, rows_seq, HEAD_DIM), lambda i: (i, 0, 0, 0)),
            pl.BlockSpec((width, HEAD_DIM), lambda i: (0, 0)),
            pl.BlockSpec((width, HEAD_DIM), lambda i: (0, 0)),
            pl.BlockSpec((BLOCK_LEN, PASSAGE), lambda i: (0, 0)),
        ],
        out_shape=[
            jax.ShapeDtypeStruct(both_heads.shape, jnp.bfloat16),
            jax.ShapeDtypeStruct((width, HEAD_DIM), jnp.bfloat16),
            jax.ShapeDtypeStruct((width, HEAD_DIM), jnp.bfloat16),
            jax.ShapeDtypeStruct((BLOCK_LEN, PASSAGE), jnp.float32),
        ],
        scratch_shapes=[
            pltpu.VMEM((HEAD_DIM, width), jnp.float32),
            pltpu.VMEM((HEAD_DIM, width), jnp.float32),
            pltpu.VMEM((BLOCK_LEN, width), jnp.float32),
        ],
        compiler_params=pltpu.CompilerParams(dimension_semantics=("arbitrary",)),
    )(both_heads, keys_flat, values_flat, keys_flat.T, values_flat.T, bias_wide, usable)


def reduce_groups(part):
    return lax.psum(lax.psum(part, "seq"), "dp")


def local(queries, cotangent, key_pool, value_pool, counts, neighbour_ids, rel_bias):
    token_rows = queries.shape[1]
    full_width = queries.shape[2]
    blocks_here = token_rows // BLOCK_LEN
    head_width = key_pool.shape[-1]
    heads_total = full_width // HEAD_DIM
    pool_size = key_pool.shape[2]
    pool_keys = key_pool.reshape(pool_size, PASSAGE, head_width)
    pool_values = value_pool.reshape(pool_size, PASSAGE, head_width)
    id_table = neighbour_ids.reshape(-1, neighbour_ids.shape[-1])
    count_table = counts.reshape(-1)
    row_bias = bias_rows(rel_bias)
    score_scale = 1.0 / math.sqrt(HEAD_DIM)
    both_rows = pl.pallas_call(
        split_kernel,
        in_specs=[pl.BlockSpec(memory_space=pl.ANY), pl.BlockSpec(memory_space=pl.ANY)],
        out_specs=pl.BlockSpec(memory_space=pl.ANY),
        scratch_shapes=[pltpu.SemaphoreType.DMA((heads_total, 2))],
        out_shape=jax.ShapeDtypeStruct((heads_total, 2, token_rows, HEAD_DIM), queries.dtype),
    )(queries.reshape(token_rows, full_width), cotangent.reshape(token_rows, full_width))
    both_heads = lax.all_to_all(both_rows, "enc", split_axis=0, concat_axis=0, tiled=True)
    both_out, key_total, value_total, bias_total = attend_all(
        both_heads, id_table, count_table, pool_keys, pool_values, row_bias
    )
    both_back = lax.all_to_all(both_out, "enc", split_axis=0, concat_axis=0, tiled=True)
    both_back = both_back.transpose(1, 2, 0, 3).reshape((2,) + queries.shape)
    bias_grad = reduce_groups(fold_bias(bias_total[None], rel_bias.shape[1]))
    return (
        both_back[0],
        both_back[1],
        key_total.reshape(key_pool.shape),
        value_total.reshape(value_pool.shape),
        bias_grad,
    )


def solution(mesh):
    in_specs = (
        P(("dp", "enc"), "seq", None),
        P(("dp", "enc"), "seq", None),
        P("dp", "seq", None, None, "enc"),
        P("dp", "seq", None, None, "enc"),
        P("dp", "seq"),
        P("dp", "seq", None),
        P("enc", None),
    )
    out_specs = (
        P(("dp", "enc"), "seq", None),
        P(("dp", "enc"), "seq", None),
        P("dp", "seq", None, None, "enc"),
        P("dp", "seq", None, None, "enc"),
        P("enc", None),
    )
    return jax.shard_map(local, mesh=mesh, in_specs=in_specs, out_specs=out_specs, check_vma=False)
```

```python
import math

import jax
import jax.numpy as jnp
from jax import lax
from jax.experimental import pallas as pl
from jax.experimental.pallas import tpu as pltpu
from jax.sharding import PartitionSpec as P

HEAD_DIM = 128
BLOCK_LEN = 64
PASSAGE = 128


NEG_FILL = -1e30


def bias_rows(bias_table):
    heads_here, table_width = bias_table.shape
    padded = jnp.pad(bias_table, ((0, 0), (0, 1)))
    tiled_rows = jnp.broadcast_to(padded[:, None, :], (heads_here, BLOCK_LEN, table_width + 1))
    tiled_rows = tiled_rows.reshape(heads_here, BLOCK_LEN * (table_width + 1))[
        :, : BLOCK_LEN * table_width
    ]
    tiled_rows = tiled_rows.reshape(heads_here, BLOCK_LEN, table_width)
    return tiled_rows[:, :, BLOCK_LEN - 1 : BLOCK_LEN - 1 + PASSAGE]


def fold_bias(totals, table_width):
    heads_here = totals.shape[0]
    padded = jnp.pad(totals, ((0, 0), (0, 0), (BLOCK_LEN - 1, 0)))
    flat_rows = padded.reshape(heads_here, BLOCK_LEN * table_width)
    flat_rows = jnp.pad(flat_rows, ((0, 0), (0, BLOCK_LEN)))
    return flat_rows.reshape(heads_here, BLOCK_LEN, table_width + 1).sum(axis=1)[:, :table_width]


def split_kernel(query_ref, grad_ref, out_ref):
    for head in range(out_ref.shape[0]):
        columns = slice(head * HEAD_DIM, (head + 1) * HEAD_DIM)
        out_ref[head, 0] = query_ref[:, columns]
        out_ref[head, 1] = grad_ref[:, columns]


def attend_kernel(qd_ref, keys_ref, values_ref, keys_t_ref, values_t_ref, bias_ref, mask_ref, out_ref, key_out, value_out,
                  bias_out, key_acc, value_acc, bias_acc):
    step = pl.program_id(0)
    score_scale = 1.0 / math.sqrt(HEAD_DIM)
    seqs_here, halves, rows_seq, _ = qd_ref.shape
    blocks_seq = rows_seq // BLOCK_LEN
    rows = seqs_here * rows_seq
    width = keys_t_ref.shape[1]
    tile4 = (seqs_here, blocks_seq, BLOCK_LEN, width)
    contract_first = (((0,), (0,)), ((), ()))

    @pl.when(step == 0)
    def _():
        key_acc[...] = jnp.zeros_like(key_acc)
        value_acc[...] = jnp.zeros_like(value_acc)
        bias_acc[...] = jnp.zeros_like(bias_acc)

    query_rows = qd_ref[:, 0].reshape(rows, HEAD_DIM)
    grad_rows = qd_ref[:, 1].reshape(rows, HEAD_DIM)
    keys = keys_ref[...]
    values = values_ref[...]
    scores = jnp.dot(query_rows, keys_t_ref[...], preferred_element_type=jnp.float32)
    scores = scores.reshape(tile4) * score_scale + bias_ref[...][None, None]
    usable = mask_ref[...][:, :, None, :] > 0.5
    masked = jnp.where(usable, scores, NEG_FILL)
    row_top = jnp.max(masked, axis=3, keepdims=True)
    raised = jnp.exp(masked - row_top)
    total = jnp.sum(raised, axis=3, keepdims=True)
    any_used = jnp.max(mask_ref[...], axis=2, keepdims=True)[:, :, :, None] > 0.5
    row_scale = jnp.where(any_used, 1.0 / total, 0.0)
    weights = raised * row_scale
    weights_low = weights.astype(jnp.bfloat16).reshape(rows, width)
    context = jnp.dot(weights_low, values, preferred_element_type=jnp.float32)
    grad_weights = jnp.dot(grad_rows, values_t_ref[...], preferred_element_type=jnp.float32)
    grad_weights = grad_weights.reshape(tile4)
    row_delta = jnp.sum(weights * grad_weights, axis=3, keepdims=True)
    grad_scores = weights * (grad_weights - row_delta)
    scores_low = grad_scores.astype(jnp.bfloat16).reshape(rows, width)
    query_grad = score_scale * jnp.dot(scores_low, keys, preferred_element_type=jnp.float32)
    out_ref[:, 0] = context.astype(jnp.bfloat16).reshape(seqs_here, rows_seq, HEAD_DIM)
    out_ref[:, 1] = query_grad.astype(jnp.bfloat16).reshape(seqs_here, rows_seq, HEAD_DIM)
    key_acc[...] += lax.dot_general(query_rows, scores_low, contract_first, preferred_element_type=jnp.float32)
    value_acc[...] += lax.dot_general(grad_rows, weights_low, contract_first, preferred_element_type=jnp.float32)
    bias_acc[...] += jnp.sum(grad_scores, axis=(0, 1))

    @pl.when(step == pl.num_programs(0) - 1)
    def _():
        key_out[...] = (score_scale * key_acc[...]).T.astype(key_out.dtype)
        value_out[...] = value_acc[...].T.astype(value_out.dtype)
        folded = bias_acc[:, 0:PASSAGE]
        for part in range(1, width // PASSAGE):
            folded = folded + bias_acc[:, part * PASSAGE:(part + 1) * PASSAGE]
        bias_out[...] = folded


def attend_all(both_heads, id_table, count_table, pool_keys, pool_values, row_bias):
    seq_total, halves, rows_seq, _ = both_heads.shape
    pool_size = pool_keys.shape[0]
    width = pool_size * PASSAGE
    blocks_seq = rows_seq // BLOCK_LEN
    keys_flat = pool_keys.reshape(width, HEAD_DIM)
    values_flat = pool_values.reshape(width, HEAD_DIM)
    slot_index = jnp.arange(id_table.shape[1])
    picked = (slot_index[None, :] < count_table[:, None])[:, :, None] & (
        id_table[:, :, None] == jnp.arange(pool_size)[None, None, :]
    )
    usable = jnp.repeat(jnp.any(picked, axis=1).astype(jnp.float32), PASSAGE, axis=1)
    usable = usable.reshape(seq_total, blocks_seq, width)
    bias_wide = jnp.tile(row_bias[0], (1, pool_size))
    seqs_step = 8
    grid = (seq_total // seqs_step,)
    return pl.pallas_call(
        attend_kernel,
        grid=grid,
        in_specs=[
            pl.BlockSpec((seqs_step, halves, rows_seq, HEAD_DIM), lambda i: (i, 0, 0, 0)),
            pl.BlockSpec((width, HEAD_DIM), lambda i: (0, 0)),
            pl.BlockSpec((width, HEAD_DIM), lambda i: (0, 0)),
            pl.BlockSpec((HEAD_DIM, width), lambda i: (0, 0)),
            pl.BlockSpec((HEAD_DIM, width), lambda i: (0, 0)),
            pl.BlockSpec((BLOCK_LEN, width), lambda i: (0, 0)),
            pl.BlockSpec((seqs_step, blocks_seq, width), lambda i: (i, 0, 0)),
        ],
        out_specs=[
            pl.BlockSpec((seqs_step, halves, rows_seq, HEAD_DIM), lambda i: (i, 0, 0, 0)),
            pl.BlockSpec((width, HEAD_DIM), lambda i: (0, 0)),
            pl.BlockSpec((width, HEAD_DIM), lambda i: (0, 0)),
            pl.BlockSpec((BLOCK_LEN, PASSAGE), lambda i: (0, 0)),
        ],
        out_shape=[
            jax.ShapeDtypeStruct(both_heads.shape, jnp.bfloat16),
            jax.ShapeDtypeStruct((width, HEAD_DIM), jnp.bfloat16),
            jax.ShapeDtypeStruct((width, HEAD_DIM), jnp.bfloat16),
            jax.ShapeDtypeStruct((BLOCK_LEN, PASSAGE), jnp.float32),
        ],
        scratch_shapes=[
            pltpu.VMEM((HEAD_DIM, width), jnp.float32),
            pltpu.VMEM((HEAD_DIM, width), jnp.float32),
            pltpu.VMEM((BLOCK_LEN, width), jnp.float32),
        ],
        compiler_params=pltpu.CompilerParams(dimension_semantics=("arbitrary",)),
    )(both_heads, keys_flat, values_flat, keys_flat.T, values_flat.T, bias_wide, usable)


def reduce_groups(part):
    return lax.psum(lax.psum(part, "seq"), "dp")


def local(queries, cotangent, key_pool, value_pool, counts, neighbour_ids, rel_bias):
    token_rows = queries.shape[1]
    full_width = queries.shape[2]
    blocks_here = token_rows // BLOCK_LEN
    head_width = key_pool.shape[-1]
    heads_total = full_width // HEAD_DIM
    pool_size = key_pool.shape[2]
    pool_keys = key_pool.reshape(pool_size, PASSAGE, head_width)
    pool_values = value_pool.reshape(pool_size, PASSAGE, head_width)
    id_table = neighbour_ids.reshape(-1, neighbour_ids.shape[-1])
    count_table = counts.reshape(-1)
    row_bias = bias_rows(rel_bias)
    score_scale = 1.0 / math.sqrt(HEAD_DIM)
    split_rows = BLOCK_LEN
    both_rows = pl.pallas_call(
        split_kernel,
        grid=(token_rows // split_rows,),
        in_specs=[pl.BlockSpec((split_rows, full_width), lambda i: (i, 0))] * 2,
        out_specs=pl.BlockSpec((heads_total, 2, split_rows, HEAD_DIM), lambda i: (0, 0, i, 0)),
        out_shape=jax.ShapeDtypeStruct((heads_total, 2, token_rows, HEAD_DIM), queries.dtype),
    )(queries.reshape(token_rows, full_width), cotangent.reshape(token_rows, full_width))
    both_heads = lax.all_to_all(both_rows, "enc", split_axis=0, concat_axis=0, tiled=True)
    both_out, key_total, value_total, bias_total = attend_all(
        both_heads, id_table, count_table, pool_keys, pool_values, row_bias
    )
    both_back = lax.all_to_all(both_out, "enc", split_axis=0, concat_axis=0, tiled=True)
    both_back = both_back.transpose(1, 2, 0, 3).reshape((2,) + queries.shape)
    bias_grad = reduce_groups(fold_bias(bias_total[None], rel_bias.shape[1]))
    return (
        both_back[0],
        both_back[1],
        key_total.reshape(key_pool.shape),
        value_total.reshape(value_pool.shape),
        bias_grad,
    )


def solution(mesh):
    in_specs = (
        P(("dp", "enc"), "seq", None),
        P(("dp", "enc"), "seq", None),
        P("dp", "seq", None, None, "enc"),
        P("dp", "seq", None, None, "enc"),
        P("dp", "seq"),
        P("dp", "seq", None),
        P("enc", None),
    )
    out_specs = (
        P(("dp", "enc"), "seq", None),
        P(("dp", "enc"), "seq", None),
        P("dp", "seq", None, None, "enc"),
        P("dp", "seq", None, None, "enc"),
        P("enc", None),
    )
    return jax.shard_map(local, mesh=mesh, in_specs=in_specs, out_specs=out_specs, check_vma=False)
```

```python
import math

import jax
import jax.numpy as jnp
from jax import lax
from jax.experimental import pallas as pl
from jax.experimental.pallas import tpu as pltpu
from jax.sharding import PartitionSpec as P

HEAD_DIM = 128
BLOCK_LEN = 64
PASSAGE = 128


NEG_FILL = -1e30


def bias_rows(bias_table):
    heads_here, table_width = bias_table.shape
    padded = jnp.pad(bias_table, ((0, 0), (0, 1)))
    tiled_rows = jnp.broadcast_to(padded[:, None, :], (heads_here, BLOCK_LEN, table_width + 1))
    tiled_rows = tiled_rows.reshape(heads_here, BLOCK_LEN * (table_width + 1))[
        :, : BLOCK_LEN * table_width
    ]
    tiled_rows = tiled_rows.reshape(heads_here, BLOCK_LEN, table_width)
    return tiled_rows[:, :, BLOCK_LEN - 1 : BLOCK_LEN - 1 + PASSAGE]


def fold_bias(totals, table_width):
    heads_here = totals.shape[0]
    padded = jnp.pad(totals, ((0, 0), (0, 0), (BLOCK_LEN - 1, 0)))
    flat_rows = padded.reshape(heads_here, BLOCK_LEN * table_width)
    flat_rows = jnp.pad(flat_rows, ((0, 0), (0, BLOCK_LEN)))
    return flat_rows.reshape(heads_here, BLOCK_LEN, table_width + 1).sum(axis=1)[:, :table_width]


def split_kernel(query_ref, grad_ref, out_ref):
    for head in range(out_ref.shape[0]):
        columns = slice(head * HEAD_DIM, (head + 1) * HEAD_DIM)
        out_ref[head, 0] = query_ref[:, columns]
        out_ref[head, 1] = grad_ref[:, columns]


def attend_kernel(qd_ref, keys_ref, values_ref, keys_t_ref, values_t_ref, bias_ref, mask_ref, out_ref, key_out, value_out,
                  bias_out, key_acc, value_acc, bias_acc):
    step = pl.program_id(0)
    score_scale = 1.0 / math.sqrt(HEAD_DIM)
    seqs_here, halves, rows_seq, _ = qd_ref.shape
    blocks_seq = rows_seq // BLOCK_LEN
    rows = seqs_here * rows_seq
    width = keys_t_ref.shape[1]
    tile4 = (seqs_here, blocks_seq, BLOCK_LEN, width)
    contract_first = (((0,), (0,)), ((), ()))

    @pl.when(step == 0)
    def _():
        key_acc[...] = jnp.zeros_like(key_acc)
        value_acc[...] = jnp.zeros_like(value_acc)
        bias_acc[...] = jnp.zeros_like(bias_acc)

    query_rows = qd_ref[:, 0].reshape(rows, HEAD_DIM)
    grad_rows = qd_ref[:, 1].reshape(rows, HEAD_DIM)
    keys = keys_ref[...]
    values = values_ref[...]
    scores = jnp.dot(query_rows, keys_t_ref[...], preferred_element_type=jnp.float32)
    scores = scores.reshape(tile4) * score_scale + bias_ref[...][None, None]
    usable = mask_ref[...][:, :, None, :] > 0.5
    masked = jnp.where(usable, scores, NEG_FILL)
    row_top = jnp.max(masked, axis=3, keepdims=True)
    raised = jnp.exp(masked - row_top)
    total = jnp.sum(raised, axis=3, keepdims=True)
    any_used = jnp.max(mask_ref[...], axis=2, keepdims=True)[:, :, :, None] > 0.5
    row_scale = jnp.where(any_used, 1.0 / total, 0.0)
    weights = raised * row_scale
    weights_low = weights.astype(jnp.bfloat16).reshape(rows, width)
    context = jnp.dot(weights_low, values, preferred_element_type=jnp.float32)
    grad_weights = jnp.dot(grad_rows, values_t_ref[...], preferred_element_type=jnp.float32)
    grad_weights = grad_weights.reshape(tile4)
    row_delta = jnp.sum(weights * grad_weights, axis=3, keepdims=True)
    grad_scores = weights * (grad_weights - row_delta)
    scores_low = grad_scores.astype(jnp.bfloat16).reshape(rows, width)
    query_grad = score_scale * jnp.dot(scores_low, keys, preferred_element_type=jnp.float32)
    out_ref[:, 0] = context.astype(jnp.bfloat16).reshape(seqs_here, rows_seq, HEAD_DIM)
    out_ref[:, 1] = query_grad.astype(jnp.bfloat16).reshape(seqs_here, rows_seq, HEAD_DIM)
    key_acc[...] += lax.dot_general(query_rows, scores_low, contract_first, preferred_element_type=jnp.float32)
    value_acc[...] += lax.dot_general(grad_rows, weights_low, contract_first, preferred_element_type=jnp.float32)
    bias_acc[...] += jnp.sum(grad_scores, axis=(0, 1))

    @pl.when(step == pl.num_programs(0) - 1)
    def _():
        key_out[...] = (score_scale * key_acc[...]).T.astype(key_out.dtype)
        value_out[...] = value_acc[...].T.astype(value_out.dtype)
        folded = bias_acc[:, 0:PASSAGE]
        for part in range(1, width // PASSAGE):
            folded = folded + bias_acc[:, part * PASSAGE:(part + 1) * PASSAGE]
        bias_out[...] = folded


def attend_all(both_heads, id_table, count_table, pool_keys, pool_values, row_bias):
    seq_total, halves, rows_seq, _ = both_heads.shape
    pool_size = pool_keys.shape[0]
    width = pool_size * PASSAGE
    blocks_seq = rows_seq // BLOCK_LEN
    keys_flat = pool_keys.reshape(width, HEAD_DIM)
    values_flat = pool_values.reshape(width, HEAD_DIM)
    slot_index = jnp.arange(id_table.shape[1])
    picked = (slot_index[None, :] < count_table[:, None])[:, :, None] & (
        id_table[:, :, None] == jnp.arange(pool_size)[None, None, :]
    )
    usable = jnp.repeat(jnp.any(picked, axis=1).astype(jnp.float32), PASSAGE, axis=1)
    usable = usable.reshape(seq_total, blocks_seq, width)
    bias_wide = jnp.tile(row_bias[0], (1, pool_size))
    seqs_step = 8
    grid = (seq_total // seqs_step,)
    return pl.pallas_call(
        attend_kernel,
        grid=grid,
        in_specs=[
            pl.BlockSpec((seqs_step, halves, rows_seq, HEAD_DIM), lambda i: (i, 0, 0, 0)),
            pl.BlockSpec((width, HEAD_DIM), lambda i: (0, 0)),
            pl.BlockSpec((width, HEAD_DIM), lambda i: (0, 0)),
            pl.BlockSpec((HEAD_DIM, width), lambda i: (0, 0)),
            pl.BlockSpec((HEAD_DIM, width), lambda i: (0, 0)),
            pl.BlockSpec((BLOCK_LEN, width), lambda i: (0, 0)),
            pl.BlockSpec((seqs_step, blocks_seq, width), lambda i: (i, 0, 0)),
        ],
        out_specs=[
            pl.BlockSpec((seqs_step, halves, rows_seq, HEAD_DIM), lambda i: (i, 0, 0, 0)),
            pl.BlockSpec((width, HEAD_DIM), lambda i: (0, 0)),
            pl.BlockSpec((width, HEAD_DIM), lambda i: (0, 0)),
            pl.BlockSpec((BLOCK_LEN, PASSAGE), lambda i: (0, 0)),
        ],
        out_shape=[
            jax.ShapeDtypeStruct(both_heads.shape, jnp.bfloat16),
            jax.ShapeDtypeStruct((width, HEAD_DIM), jnp.bfloat16),
            jax.ShapeDtypeStruct((width, HEAD_DIM), jnp.bfloat16),
            jax.ShapeDtypeStruct((BLOCK_LEN, PASSAGE), jnp.float32),
        ],
        scratch_shapes=[
            pltpu.VMEM((HEAD_DIM, width), jnp.float32),
            pltpu.VMEM((HEAD_DIM, width), jnp.float32),
            pltpu.VMEM((BLOCK_LEN, width), jnp.float32),
        ],
        compiler_params=pltpu.CompilerParams(dimension_semantics=("arbitrary",)),
    )(both_heads, keys_flat, values_flat, keys_flat.T, values_flat.T, bias_wide, usable)


def reduce_groups(part):
    return lax.psum(lax.psum(part, "seq"), "dp")


def local(queries, cotangent, key_pool, value_pool, counts, neighbour_ids, rel_bias):
    token_rows = queries.shape[1]
    full_width = queries.shape[2]
    blocks_here = token_rows // BLOCK_LEN
    head_width = key_pool.shape[-1]
    heads_total = full_width // HEAD_DIM
    pool_size = key_pool.shape[2]
    pool_keys = key_pool.reshape(pool_size, PASSAGE, head_width)
    pool_values = value_pool.reshape(pool_size, PASSAGE, head_width)
    id_table = neighbour_ids.reshape(-1, neighbour_ids.shape[-1])
    count_table = counts.reshape(-1)
    row_bias = bias_rows(rel_bias)
    score_scale = 1.0 / math.sqrt(HEAD_DIM)
    split_rows = BLOCK_LEN // 2
    both_rows = pl.pallas_call(
        split_kernel,
        grid=(token_rows // split_rows,),
        in_specs=[pl.BlockSpec((split_rows, full_width), lambda i: (i, 0))] * 2,
        out_specs=pl.BlockSpec((heads_total, 2, split_rows, HEAD_DIM), lambda i: (0, 0, i, 0)),
        out_shape=jax.ShapeDtypeStruct((heads_total, 2, token_rows, HEAD_DIM), queries.dtype),
    )(queries.reshape(token_rows, full_width), cotangent.reshape(token_rows, full_width))
    both_heads = lax.all_to_all(both_rows, "enc", split_axis=0, concat_axis=0, tiled=True)
    both_out, key_total, value_total, bias_total = attend_all(
        both_heads, id_table, count_table, pool_keys, pool_values, row_bias
    )
    both_back = lax.all_to_all(both_out, "enc", split_axis=0, concat_axis=0, tiled=True)
    both_back = both_back.transpose(1, 2, 0, 3).reshape((2,) + queries.shape)
    bias_grad = reduce_groups(fold_bias(bias_total[None], rel_bias.shape[1]))
    return (
        both_back[0],
        both_back[1],
        key_total.reshape(key_pool.shape),
        value_total.reshape(value_pool.shape),
        bias_grad,
    )


def solution(mesh):
    in_specs = (
        P(("dp", "enc"), "seq", None),
        P(("dp", "enc"), "seq", None),
        P("dp", "seq", None, None, "enc"),
        P("dp", "seq", None, None, "enc"),
        P("dp", "seq"),
        P("dp", "seq", None),
        P("enc", None),
    )
    out_specs = (
        P(("dp", "enc"), "seq", None),
        P(("dp", "enc"), "seq", None),
        P("dp", "seq", None, None, "enc"),
        P("dp", "seq", None, None, "enc"),
        P("enc", None),
    )
    return jax.shard_map(local, mesh=mesh, in_specs=in_specs, out_specs=out_specs, check_vma=False)
```
